512 devices in a mesh: outer: 16 (over y, z_hi, core), inner: 32 (over x, z_lo).
Axes of the slice: x: 4, y: 4, z: 16 (z_hi: 2, z_lo: 8; z = z_hi * 8 + z_lo), core: 2. Of those that a mesh axis runs over, the one named last changes fastest.
Arguments:
- signal: bfloat16 [524288, 256], P(('outer', 'inner')), may hold values from -6 to 6
- conv_past: bfloat16 [2, 256, 512], replicated, may hold values from -0.25 to 0.25
- conv_now: bfloat16 [2, 256, 512], replicated, may hold values from -0.25 to 0.25
- out_proj: bfloat16 [2, 256, 256], replicated, may hold values from -0.375 to 0.375
- cotangent: bfloat16 [524288, 256], P(('outer', 'inner')), may hold values from -6 to 6
Outputs:
- result: bfloat16 [524288, 256], P(('outer', 'inner'))
- grad_signal: bfloat16 [524288, 256], P(('outer', 'inner'))
- grad_past: float32 [2, 256, 512], P(None, 'inner')
- grad_now: float32 [2, 256, 512], P(None, 'inner')
- grad_out: float32 [2, 256, 256], P(None, 'inner')
The draws below stay inside these ranges and needn't reach their ends.
All inputs are finite; a program needn't handle non-finite values.
Results may differ from the reference program's by a relative error of at most 0.0056.
Values may be sent and summed in bfloat16 or wider, within the bound.
No kernel may reach another device: no remote copies, remote signals or barrier semaphores. Data moves between devices by JAX's collectives and lax.ppermute only.
A program may use at most 64 MiB of HBM per device.

```python
import math
import jax
import jax.numpy as jnp
from jax import lax

C = 256
G = 512
TD = 1024
LAYERS = 2
TICKS = 524288
N_INNER = 32


def block_scale(own_key, extent, shards, least, largest):
    level, own = 1.0, jax.random.fold_in(own_key, 6)
    for axis_at, shards_of in shards:
        draws = jnp.exp(jax.random.uniform(jax.random.fold_in(own, axis_at), (shards_of,), jnp.float32, least / len(shards), largest / len(shards)))
        level = level * jnp.repeat(draws, extent[axis_at] // shards_of).reshape([-1 if axis == axis_at else 1 for axis in range(len(extent))])
    return level


def normal_values(own_key, dims, spread, bound, shards=(), held_as=jnp.bfloat16):
    drawn = jax.random.normal(own_key, dims, jnp.float32) * spread
    if len(shards) > 0:
        drawn = block_scale(own_key, dims, shards, -0.22, 0.18) * drawn
    return jnp.clip(drawn, min=-bound, max=bound).astype(held_as)


def setup_inputs(seed: int = 0) -> dict:
    seeds = jax.random.split(jax.random.key(seed), 6)
    return {
        "signal": normal_values(seeds[0], (TICKS, C), 1.0, 6.0, ((0, 512),)),
        "conv_past": normal_values(seeds[1], (LAYERS, C, G), (2 * C) ** -0.5, 0.25),
        "conv_now": normal_values(seeds[2], (LAYERS, C, G), (2 * C) ** -0.5, 0.25),
        "out_proj": normal_values(seeds[3], (LAYERS, C, C), C ** -0.5, 0.375),
        "cotangent": normal_values(seeds[4], (TICKS, C), 1.0, 6.0, ((0, 512),)),
    }


def delayed(series, offset):
    zero_rows = jnp.zeros((offset, series.shape[1]), series.dtype)
    return jnp.concatenate([zero_rows, series[:-offset]], 0)

def advanced(series, offset):
    zero_rows = jnp.zeros((offset, series.shape[1]), series.dtype)
    return jnp.concatenate([series[offset:], zero_rows], 0)

def blocks(series, block_rows):
    return series.reshape((series.shape[0] // block_rows, block_rows) + series.shape[1:])

def gating(current, earlier, w_past, w_now):
    preact = jnp.dot(earlier, w_past, preferred_element_type=jnp.float32) + jnp.dot(current, w_now, preferred_element_type=jnp.float32)
    half_width = preact.shape[1] // 2
    return (jnp.tanh(preact[:, :half_width]), jax.nn.sigmoid(preact[:, half_width:]))

def reference(signal, conv_past, conv_now, out_proj, cotangent):
    tick_count = signal.shape[0]
    channels = signal.shape[1]
    gate_width = conv_past.shape[2]
    block_rows = min(tick_count, 8192)
    lag_list = (TD, 2 * TD * N_INNER)
    states = [signal]
    current = signal
    for layer_at in range(LAYERS):
        earlier = delayed(current, lag_list[layer_at])

        def forward(inputs_pair, layer_at=layer_at):
            cur_block, old_block = inputs_pair
            tanh_part, sig_part = gating(cur_block, old_block, conv_past[layer_at], conv_now[layer_at])
            gated_out = (tanh_part * sig_part).astype(jnp.bfloat16)
            return (cur_block.astype(jnp.float32) + jnp.dot(gated_out, out_proj[layer_at], preferred_element_type=jnp.float32)).astype(jnp.bfloat16)
        current = lax.map(forward, (blocks(current, block_rows), blocks(earlier, block_rows))).reshape(tick_count, channels)
        states.append(current)
    result = current
    grad_scale = 1.0 / math.sqrt(tick_count)
    upstream = cotangent
    past_list, now_list, out_list = ([], [], [])
    for layer_at in reversed(range(LAYERS)):
        offset = lag_list[layer_at]
        current = states[layer_at]
        earlier = delayed(current, offset)

        def backward(summed, block_inputs, layer_at=layer_at):
            cur_block, old_block, up_block = block_inputs
            tanh_part, sig_part = gating(cur_block, old_block, conv_past[layer_at], conv_now[layer_at])
            gated_out = (tanh_part * sig_part).astype(jnp.bfloat16)
            grad_gated = jnp.dot(up_block, out_proj[layer_at].T, preferred_element_type=jnp.float32)
            grad_filter = grad_gated * sig_part * (1.0 - tanh_part * tanh_part)
            grad_gate = grad_gated * tanh_part * sig_part * (1.0 - sig_part)
            grad_preact = jnp.concatenate([grad_filter, grad_gate], 1).astype(jnp.bfloat16)
            weight_term = jnp.concatenate([jnp.dot(old_block.T, grad_preact, preferred_element_type=jnp.float32), jnp.dot(cur_block.T, grad_preact, preferred_element_type=jnp.float32), jnp.dot(gated_out.T, up_block, preferred_element_type=jnp.float32)], 1)
            local_grad = up_block.astype(jnp.float32) + jnp.dot(grad_preact, conv_now[layer_at].T, preferred_element_type=jnp.float32)
            sent_back = jnp.dot(grad_preact, conv_past[layer_at].T, preferred_element_type=jnp.float32).astype(jnp.bfloat16)
            return (summed + weight_term, (local_grad, sent_back))
        start_sum = jnp.zeros((channels, 2 * gate_width + channels), jnp.float32)
        summed, (local_grad, sent_back) = lax.scan(backward, start_sum, (blocks(current, block_rows), blocks(earlier, block_rows), blocks(upstream, block_rows)))
        local_grad = local_grad.reshape(tick_count, channels)
        sent_back = sent_back.reshape(tick_count, channels)
        upstream = (local_grad + advanced(sent_back, offset).astype(jnp.float32)).astype(jnp.bfloat16)
        summed = summed * grad_scale
        past_list.insert(0, summed[:, :gate_width])
        now_list.insert(0, summed[:, gate_width:2 * gate_width])
        out_list.insert(0, summed[:, 2 * gate_width:])
    return (result, upstream, jnp.stack(past_list), jnp.stack(now_list), jnp.stack(out_list))
```

```python
import math

import jax
import jax.numpy as jnp
from jax import lax
from jax.sharding import Mesh
from jax.sharding import PartitionSpec as P

OUTER = ("y", "z_hi", "core")
INNER = ("x", "z_lo")
EVERY = OUTER + INNER


def group_size(axes):
    size = 1
    for axis in axes:
        size *= lax.axis_size(axis)
    return size


def group_index(axes):
    index = 0
    for axis in axes:
        index = index * lax.axis_size(axis) + lax.axis_index(axis)
    return index


def from_behind(array, axes, by):
    size = group_size(axes)
    pairs = [(i, i + by) for i in range(size) if 0 <= i + by < size]
    return lax.ppermute(array, axes, pairs)


def scatter_sum(total, axes):
    size = group_size(axes)
    own = group_index(axes)
    pieces = total.reshape(size, total.shape[0] // size, *total.shape[1:])
    summed = lax.dynamic_index_in_dim(pieces, own, 0, keepdims=False)
    for shift in range(1, size):
        piece = lax.dynamic_index_in_dim(pieces, (own + shift) % size, 0, keepdims=False)
        summed = summed + lax.ppermute(piece, axes, [(i, (i + shift) % size) for i in range(size)])
    return summed


def everyone_sum(total, axes):
    size = group_size(axes)
    step = 1
    while step < size:
        total = total + lax.ppermute(total, axes, [(i, i ^ step) for i in range(size)])
        step *= 2
    return total


def weight_sum(term):
    for axis in INNER:
        term = scatter_sum(term, (axis,))
    return everyone_sum(term, OUTER)


def gating(current, earlier, w_past, w_now):
    preact = jnp.dot(earlier, w_past, preferred_element_type=jnp.float32) + jnp.dot(
        current, w_now, preferred_element_type=jnp.float32
    )
    half_width = preact.shape[1] // 2
    return (jnp.tanh(preact[:, :half_width]), jax.nn.sigmoid(preact[:, half_width:]))


def fetch_past(series, layer_at):
    if layer_at == 0:
        return from_behind(series, EVERY, 1)
    return from_behind(series, OUTER, 2)


def return_past(series, layer_at):
    if layer_at == 0:
        return from_behind(series, EVERY, -1)
    return from_behind(series, OUTER, -2)


def layer_term(operands, grad_scale):
    earlier, current, gated_out, grad_preact, upstream = operands

    def contract(left_op, right_op):
        return lax.dot_general(
            left_op, right_op, (((0,), (0,)), ((), ())), preferred_element_type=jnp.float32
        )

    return (
        jnp.concatenate(
            [
                contract(earlier, grad_preact),
                contract(current, grad_preact),
                contract(gated_out, upstream),
            ],
            1,
        )
        * grad_scale
    )


def local(signal, conv_past, conv_now, out_proj, cotangent):
    gate_width = conv_past.shape[2]
    tick_count = signal.shape[0] * group_size(EVERY)
    grad_scale = 1.0 / math.sqrt(tick_count)
    layer_count = conv_past.shape[0]
    inputs, earliers, saved = ([], [], [])
    current = signal
    for layer_at in range(layer_count):
        earlier = fetch_past(current, layer_at)
        tanh_part, sig_part = gating(current, earlier, conv_past[layer_at], conv_now[layer_at])
        gated_out = (tanh_part * sig_part).astype(jnp.bfloat16)
        inputs.append(current)
        earliers.append(earlier)
        saved.append((tanh_part, sig_part, gated_out))
        current = (
            current.astype(jnp.float32)
            + jnp.dot(gated_out, out_proj[layer_at], preferred_element_type=jnp.float32)
        ).astype(jnp.bfloat16)
    result = current
    upstream = cotangent
    summed_list = [None] * layer_count
    for layer_at in reversed(range(layer_count)):
        current = inputs[layer_at]
        earlier = earliers[layer_at]
        tanh_part, sig_part, gated_out = saved[layer_at]
        grad_gated = jnp.dot(upstream, out_proj[layer_at].T, preferred_element_type=jnp.float32)
        grad_filter = grad_gated * sig_part * (1.0 - tanh_part * tanh_part)
        grad_gate = grad_gated * tanh_part * sig_part * (1.0 - sig_part)
        grad_preact = jnp.concatenate([grad_filter, grad_gate], 1).astype(jnp.bfloat16)
        sent_back = jnp.dot(
            grad_preact, conv_past[layer_at].T, preferred_element_type=jnp.float32
        ).astype(jnp.bfloat16)
        arrived = return_past(sent_back, layer_at)
        operands = (earlier, current, gated_out, grad_preact, upstream)
        summed_list[layer_at] = weight_sum(layer_term(operands, grad_scale))
        local_grad = upstream.astype(jnp.float32) + jnp.dot(
            grad_preact, conv_now[layer_at].T, preferred_element_type=jnp.float32
        )
        upstream = (local_grad + arrived.astype(jnp.float32)).astype(jnp.bfloat16)
    past_list = [summed[:, :gate_width] for summed in summed_list]
    now_list = [summed[:, gate_width : 2 * gate_width] for summed in summed_list]
    out_list = [summed[:, 2 * gate_width :] for summed in summed_list]
    return (result, upstream, jnp.stack(past_list), jnp.stack(now_list), jnp.stack(out_list))


def solution(mesh):
    outer_size = mesh.shape["outer"]
    inner_size = mesh.shape["inner"]
    split = Mesh(
        mesh.devices.reshape(outer_size // 4, 2, 2, inner_size // 8, 8),
        ("y", "z_hi", "core", "x", "z_lo"),
    )
    placed = (P(EVERY, None), P(), P(), P(), P(EVERY, None))
    return jax.shard_map(
        local,
        mesh=split,
        in_specs=placed,
        out_specs=(
            P(EVERY, None),
            P(EVERY, None),
            P(None, INNER, None),
            P(None, INNER, None),
            P(None, INNER, None),
        ),
        check_vma=False,
    )
```

```python
import math

import jax
import jax.numpy as jnp
from jax import lax
from jax.sharding import Mesh
from jax.sharding import PartitionSpec as P

OUTER = ("y", "z_hi", "core")
INNER = ("x", "z_lo")
EVERY = OUTER + INNER


def group_size(axes):
    size = 1
    for axis in axes:
        size *= lax.axis_size(axis)
    return size


def group_index(axes):
    index = 0
    for axis in axes:
        index = index * lax.axis_size(axis) + lax.axis_index(axis)
    return index


def from_behind(array, axes, by):
    size = group_size(axes)
    pairs = [(i, i + by) for i in range(size) if 0 <= i + by < size]
    return lax.ppermute(array, axes, pairs)


def scatter_sum(total, axes):
    size = group_size(axes)
    own = group_index(axes)
    pieces = total.reshape(size, total.shape[0] // size, *total.shape[1:])
    summed = lax.dynamic_index_in_dim(pieces, own, 0, keepdims=False)
    for shift in range(1, size):
        piece = lax.dynamic_index_in_dim(pieces, (own + shift) % size, 0, keepdims=False)
        summed = summed + lax.ppermute(piece, axes, [(i, (i + shift) % size) for i in range(size)])
    return summed


def halving_sum(total, axes):
    size = group_size(axes)
    own = group_index(axes)
    step = size // 2
    while step >= 1:
        halves = total.reshape(2, total.shape[0] // 2, *total.shape[1:])
        keep = (own // step) % 2
        kept = lax.dynamic_index_in_dim(halves, keep, 0, keepdims=False)
        given = lax.dynamic_index_in_dim(halves, 1 - keep, 0, keepdims=False)
        total = kept + lax.ppermute(given, axes, [(i, i ^ step) for i in range(size)])
        step //= 2
    return total


def everyone_sum(total, axes):
    size = group_size(axes)
    step = 1
    while step < size:
        total = total + lax.ppermute(total, axes, [(i, i ^ step) for i in range(size)])
        step *= 2
    return total


def weight_sum(term):
    own_core = lax.axis_index("core")
    halves = term.reshape(term.shape[0], 2, term.shape[1] // 2)
    kept = lax.dynamic_index_in_dim(halves, own_core, 1, keepdims=False)
    given = lax.dynamic_index_in_dim(halves, 1 - own_core, 1, keepdims=False)
    term = kept + lax.ppermute(given, "core", [(0, 1), (1, 0)])
    term = scatter_sum(term, ("x",))
    term = halving_sum(term, ("z_lo",))
    term = everyone_sum(term, ("y", "z_hi"))
    other = lax.ppermute(term, "core", [(0, 1), (1, 0)])
    pair = jnp.stack([term, other])
    first = lax.dynamic_index_in_dim(pair, own_core, 0, keepdims=False)
    second = lax.dynamic_index_in_dim(pair, 1 - own_core, 0, keepdims=False)
    return jnp.concatenate([first, second], 1)


def gating(current, earlier, w_past, w_now):
    preact = jnp.dot(earlier, w_past, preferred_element_type=jnp.float32) + jnp.dot(
        current, w_now, preferred_element_type=jnp.float32
    )
    half_width = preact.shape[1] // 2
    return (jnp.tanh(preact[:, :half_width]), jax.nn.sigmoid(preact[:, half_width:]))


def fetch_past(series, layer_at):
    if layer_at == 0:
        return from_behind(series, EVERY, 1)
    return from_behind(series, OUTER, 2)


def return_past(series, layer_at):
    if layer_at == 0:
        return from_behind(series, EVERY, -1)
    return from_behind(series, OUTER, -2)


def layer_term(operands, grad_scale):
    earlier, current, gated_out, grad_preact, upstream = operands

    def contract(left_op, right_op):
        return lax.dot_general(
            left_op, right_op, (((0,), (0,)), ((), ())), preferred_element_type=jnp.float32
        )

    return (
        jnp.concatenate(
            [
                contract(earlier, grad_preact),
                contract(current, grad_preact),
                contract(gated_out, upstream),
            ],
            1,
        )
        * grad_scale
    )


def local(signal, conv_past, conv_now, out_proj, cotangent):
    gate_width = conv_past.shape[2]
    tick_count = signal.shape[0] * group_size(EVERY)
    grad_scale = 1.0 / math.sqrt(tick_count)
    layer_count = conv_past.shape[0]
    inputs, earliers, saved = ([], [], [])
    current = signal
    for layer_at in range(layer_count):
        earlier = fetch_past(current, layer_at)
        tanh_part, sig_part = gating(current, earlier, conv_past[layer_at], conv_now[layer_at])
        gated_out = (tanh_part * sig_part).astype(jnp.bfloat16)
        inputs.append(current)
        earliers.append(earlier)
        saved.append((tanh_part, sig_part, gated_out))
        current = (
            current.astype(jnp.float32)
            + jnp.dot(gated_out, out_proj[layer_at], preferred_element_type=jnp.float32)
        ).astype(jnp.bfloat16)
    result = current
    upstream = cotangent
    summed_list = [None] * layer_count
    for layer_at in reversed(range(layer_count)):
        current = inputs[layer_at]
        earlier = earliers[layer_at]
        tanh_part, sig_part, gated_out = saved[layer_at]
        grad_gated = jnp.dot(upstream, out_proj[layer_at].T, preferred_element_type=jnp.float32)
        grad_filter = grad_gated * sig_part * (1.0 - tanh_part * tanh_part)
        grad_gate = grad_gated * tanh_part * sig_part * (1.0 - sig_part)
        grad_preact = jnp.concatenate([grad_filter, grad_gate], 1).astype(jnp.bfloat16)
        sent_back = jnp.dot(
            grad_preact, conv_past[layer_at].T, preferred_element_type=jnp.float32
        ).astype(jnp.bfloat16)
        arrived = return_past(sent_back, layer_at)
        operands = (earlier, current, gated_out, grad_preact, upstream)
        summed_list[layer_at] = layer_term(operands, grad_scale)
        local_grad = upstream.astype(jnp.float32) + jnp.dot(
            grad_preact, conv_now[layer_at].T, preferred_element_type=jnp.float32
        )
        upstream = (local_grad + arrived.astype(jnp.float32)).astype(jnp.bfloat16)
    term_width = summed_list[0].shape[1]
    whole = weight_sum(jnp.concatenate(summed_list, 1))
    summed_list = [
        whole[:, layer_at * term_width : (layer_at + 1) * term_width]
        for layer_at in range(layer_count)
    ]
    past_list = [summed[:, :gate_width] for summed in summed_list]
    now_list = [summed[:, gate_width : 2 * gate_width] for summed in summed_list]
    out_list = [summed[:, 2 * gate_width :] for summed in summed_list]
    return (result, upstream, jnp.stack(past_list), jnp.stack(now_list), jnp.stack(out_list))


def solution(mesh):
    outer_size = mesh.shape["outer"]
    inner_size = mesh.shape["inner"]
    split = Mesh(
        mesh.devices.reshape(outer_size // 4, 2, 2, inner_size // 8, 8),
        ("y", "z_hi", "core", "x", "z_lo"),
    )
    placed = (P(EVERY, None), P(), P(), P(), P(EVERY, None))
    return jax.shard_map(
        local,
        mesh=split,
        in_specs=placed,
        out_specs=(
            P(EVERY, None),
            P(EVERY, None),
            P(None, INNER, None),
            P(None, INNER, None),
            P(None, INNER, None),
        ),
        check_vma=False,
    )
```

```python
import math

import jax
import jax.numpy as jnp
from jax import lax
from jax.sharding import Mesh
from jax.sharding import PartitionSpec as P

OUTER = ("y", "z_hi", "core")
INNER = ("x", "z_lo")
EVERY = OUTER + INNER


def group_size(axes):
    size = 1
    for axis in axes:
        size *= lax.axis_size(axis)
    return size


def group_index(axes):
    index = 0
    for axis in axes:
        index = index * lax.axis_size(axis) + lax.axis_index(axis)
    return index


def from_behind(array, axes, by):
    size = group_size(axes)
    pairs = [(i, i + by) for i in range(size) if 0 <= i + by < size]
    return lax.ppermute(array, axes, pairs)


def scatter_sum(total, axes):
    size = group_size(axes)
    own = group_index(axes)
    pieces = total.reshape(size, total.shape[0] // size, *total.shape[1:])
    summed = lax.dynamic_index_in_dim(pieces, own, 0, keepdims=False)
    for shift in range(1, size):
        piece = lax.dynamic_index_in_dim(pieces, (own + shift) % size, 0, keepdims=False)
        summed = summed + lax.ppermute(piece, axes, [(i, (i + shift) % size) for i in range(size)])
    return summed


def halving_sum(total, axes):
    size = group_size(axes)
    own = group_index(axes)
    step = size // 2
    while step >= 1:
        halves = total.reshape(2, total.shape[0] // 2, *total.shape[1:])
        keep = (own // step) % 2
        kept = lax.dynamic_index_in_dim(halves, keep, 0, keepdims=False)
        given = lax.dynamic_index_in_dim(halves, 1 - keep, 0, keepdims=False)
        total = kept + lax.ppermute(given, axes, [(i, i ^ step) for i in range(size)])
        step //= 2
    return total


def everyone_sum(total, axes):
    size = group_size(axes)
    step = 1
    while step < size:
        total = total + lax.ppermute(total, axes, [(i, i ^ step) for i in range(size)])
        step *= 2
    return total


def near_sum(term):
    own_core = lax.axis_index("core")
    halves = term.reshape(term.shape[0], 2, term.shape[1] // 2)
    kept = lax.dynamic_index_in_dim(halves, own_core, 1, keepdims=False)
    given = lax.dynamic_index_in_dim(halves, 1 - own_core, 1, keepdims=False)
    term = kept + lax.ppermute(given, "core", [(0, 1), (1, 0)])
    return scatter_sum(term, ("x",))


def far_sum(term):
    size = lax.axis_size("z_lo")
    pieces = term.reshape(size, term.shape[0] // size, term.shape[1])
    term = lax.all_to_all(pieces, "z_lo", 0, 0, tiled=True).sum(0)
    term = everyone_sum(term, ("y", "z_hi"))
    other = lax.ppermute(term, "core", [(0, 1), (1, 0)])
    own_core = lax.axis_index("core")
    pair = jnp.stack([term, other])
    first = lax.dynamic_index_in_dim(pair, own_core, 0, keepdims=False)
    second = lax.dynamic_index_in_dim(pair, 1 - own_core, 0, keepdims=False)
    return first, second


def gating(current, earlier, w_past, w_now):
    preact = jnp.dot(earlier, w_past, preferred_element_type=jnp.float32) + jnp.dot(
        current, w_now, preferred_element_type=jnp.float32
    )
    half_width = preact.shape[1] // 2
    return (jnp.tanh(preact[:, :half_width]), jax.nn.sigmoid(preact[:, half_width:]))


def fetch_past(series, layer_at):
    if layer_at == 0:
        return from_behind(series, EVERY, 1)
    return from_behind(series, OUTER, 2)


def return_past(series, layer_at):
    if layer_at == 0:
        return from_behind(series, EVERY, -1)
    return from_behind(series, OUTER, -2)


def layer_term(operands, grad_scale):
    earlier, current, gated_out, grad_preact, upstream = operands

    def contract(left_op, right_op):
        return lax.dot_general(
            left_op, right_op, (((0,), (0,)), ((), ())), preferred_element_type=jnp.float32
        )

    return (
        jnp.concatenate(
            [
                contract(earlier, grad_preact),
                contract(current, grad_preact),
                contract(gated_out, upstream),
            ],
            1,
        )
        * grad_scale
    )


def local(signal, conv_past, conv_now, out_proj, cotangent):
    gate_width = conv_past.shape[2]
    tick_count = signal.shape[0] * group_size(EVERY)
    grad_scale = 1.0 / math.sqrt(tick_count)
    layer_count = conv_past.shape[0]
    inputs, earliers, saved = ([], [], [])
    current = signal
    for layer_at in range(layer_count):
        earlier = fetch_past(current, layer_at)
        tanh_part, sig_part = gating(current, earlier, conv_past[layer_at], conv_now[layer_at])
        gated_out = (tanh_part * sig_part).astype(jnp.bfloat16)
        inputs.append(current)
        earliers.append(earlier)
        saved.append((tanh_part, sig_part, gated_out))
        current = (
            current.astype(jnp.float32)
            + jnp.dot(gated_out, out_proj[layer_at], preferred_element_type=jnp.float32)
        ).astype(jnp.bfloat16)
    result = current
    upstream = cotangent
    near_list = [None] * layer_count
    for layer_at in reversed(range(layer_count)):
        current = inputs[layer_at]
        earlier = earliers[layer_at]
        tanh_part, sig_part, gated_out = saved[layer_at]
        grad_gated = jnp.dot(upstream, out_proj[layer_at].T, preferred_element_type=jnp.float32)
        grad_filter = grad_gated * sig_part * (1.0 - tanh_part * tanh_part)
        grad_gate = grad_gated * tanh_part * sig_part * (1.0 - sig_part)
        grad_preact = jnp.concatenate([grad_filter, grad_gate], 1).astype(jnp.bfloat16)
        sent_back = jnp.dot(
            grad_preact, conv_past[layer_at].T, preferred_element_type=jnp.float32
        ).astype(jnp.bfloat16)
        arrived = return_past(sent_back, layer_at)
        operands = (earlier, current, gated_out, grad_preact, upstream)
        near_list[layer_at] = near_sum(layer_term(operands, grad_scale))
        near_list, arrived = lax.optimization_barrier((near_list, arrived))
        local_grad = upstream.astype(jnp.float32) + jnp.dot(
            grad_preact, conv_now[layer_at].T, preferred_element_type=jnp.float32
        )
        upstream = (local_grad + arrived.astype(jnp.float32)).astype(jnp.bfloat16)
    first, second = far_sum(jnp.concatenate(near_list, 1))
    half_width = near_list[0].shape[1]
    summed_list = [
        jnp.concatenate(
            [
                first[:, layer_at * half_width : (layer_at + 1) * half_width],
                second[:, layer_at * half_width : (layer_at + 1) * half_width],
            ],
            1,
        )
        for layer_at in range(layer_count)
    ]
    past_list = [summed[:, :gate_width] for summed in summed_list]
    now_list = [summed[:, gate_width : 2 * gate_width] for summed in summed_list]
    out_list = [summed[:, 2 * gate_width :] for summed in summed_list]
    return (result, upstream, jnp.stack(past_list), jnp.stack(now_list), jnp.stack(out_list))


def solution(mesh):
    outer_size = mesh.shape["outer"]
    inner_size = mesh.shape["inner"]
    split = Mesh(
        mesh.devices.reshape(outer_size // 4, 2, 2, inner_size // 8, 8),
        ("y", "z_hi", "core", "x", "z_lo"),
    )
    placed = (P(EVERY, None), P(), P(), P(), P(EVERY, None))
    return jax.shard_map(
        local,
        mesh=split,
        in_specs=placed,
        out_specs=(
            P(EVERY, None),
            P(EVERY, None),
            P(None, INNER, None),
            P(None, INNER, None),
            P(None, INNER, None),
        ),
        check_vma=False,
    )
```

```python
import math

import jax
import jax.numpy as jnp
from jax import lax
from jax.sharding import Mesh
from jax.sharding import PartitionSpec as P

OUTER = ("y", "z_hi", "core")
INNER = ("x", "z_lo")
EVERY = OUTER + INNER


def group_size(axes):
    size = 1
    for axis in axes:
        size *= lax.axis_size(axis)
    return size


def group_index(axes):
    index = 0
    for axis in axes:
        index = index * lax.axis_size(axis) + lax.axis_index(axis)
    return index


def from_behind(array, axes, by):
    size = group_size(axes)
    pairs = [(i, i + by) for i in range(size) if 0 <= i + by < size]
    return lax.ppermute(array, axes, pairs)


def scatter_sum(total, axes):
    size = group_size(axes)
    own = group_index(axes)
    pieces = total.reshape(size, total.shape[0] // size, *total.shape[1:])
    summed = lax.dynamic_index_in_dim(pieces, own, 0, keepdims=False)
    for shift in range(1, size):
        piece = lax.dynamic_index_in_dim(pieces, (own + shift) % size, 0, keepdims=False)
        summed = summed + lax.ppermute(piece, axes, [(i, (i + shift) % size) for i in range(size)])
    return summed


def halving_sum(total, axes):
    size = group_size(axes)
    own = group_index(axes)
    step = size // 2
    while step >= 1:
        halves = total.reshape(2, total.shape[0] // 2, *total.shape[1:])
        keep = (own // step) % 2
        kept = lax.dynamic_index_in_dim(halves, keep, 0, keepdims=False)
        given = lax.dynamic_index_in_dim(halves, 1 - keep, 0, keepdims=False)
        total = kept + lax.ppermute(given, axes, [(i, i ^ step) for i in range(size)])
        step //= 2
    return total


def everyone_sum(total, axes):
    size = group_size(axes)
    step = 1
    while step < size:
        total = total + lax.ppermute(total, axes, [(i, i ^ step) for i in range(size)])
        step *= 2
    return total


def near_sum(term):
    own_core = lax.axis_index("core")
    halves = term.reshape(term.shape[0], 2, term.shape[1] // 2)
    kept = lax.dynamic_index_in_dim(halves, own_core, 1, keepdims=False)
    given = lax.dynamic_index_in_dim(halves, 1 - own_core, 1, keepdims=False)
    term = kept + lax.ppermute(given, "core", [(0, 1), (1, 0)])
    return scatter_sum(term, ("x",))


def far_sum(term):
    lo_size = lax.axis_size("z_lo")
    hi_size = lax.axis_size("y") * lax.axis_size("z_hi")
    rows = term.reshape(lo_size, hi_size, term.shape[1]).transpose(1, 0, 2)
    rows = rows.reshape(hi_size * lo_size, 1, term.shape[1])
    row = lax.all_to_all(rows, ("y", "z_hi", "z_lo"), 0, 0, tiled=True).sum(0)
    spread = jnp.broadcast_to(row[None], (hi_size, *row.shape))
    term = lax.all_to_all(spread, ("y", "z_hi"), 0, 0, tiled=True).reshape(hi_size, term.shape[1])
    other = lax.ppermute(term, "core", [(0, 1), (1, 0)])
    own_core = lax.axis_index("core")
    pair = jnp.stack([term, other])
    first = lax.dynamic_index_in_dim(pair, own_core, 0, keepdims=False)
    second = lax.dynamic_index_in_dim(pair, 1 - own_core, 0, keepdims=False)
    return first, second


def gating(current, earlier, w_past, w_now):
    preact = jnp.dot(earlier, w_past, preferred_element_type=jnp.float32) + jnp.dot(
        current, w_now, preferred_element_type=jnp.float32
    )
    half_width = preact.shape[1] // 2
    return (jnp.tanh(preact[:, :half_width]), jax.nn.sigmoid(preact[:, half_width:]))


def fetch_past(series, layer_at):
    if layer_at == 0:
        return from_behind(series, EVERY, 1)
    return from_behind(series, OUTER, 2)


def return_past(series, layer_at):
    if layer_at == 0:
        return from_behind(series, EVERY, -1)
    return from_behind(series, OUTER, -2)


def layer_term(operands, grad_scale):
    earlier, current, gated_out, grad_preact, upstream = operands

    def contract(left_op, right_op):
        return lax.dot_general(
            left_op, right_op, (((0,), (0,)), ((), ())), preferred_element_type=jnp.float32
        )

    return (
        jnp.concatenate(
            [
                contract(earlier, grad_preact),
                contract(current, grad_preact),
                contract(gated_out, upstream),
            ],
            1,
        )
        * grad_scale
    )


def local(signal, conv_past, conv_now, out_proj, cotangent):
    gate_width = conv_past.shape[2]
    tick_count = signal.shape[0] * group_size(EVERY)
    grad_scale = 1.0 / math.sqrt(tick_count)
    layer_count = conv_past.shape[0]
    inputs, earliers, saved = ([], [], [])
    current = signal
    for layer_at in range(layer_count):
        earlier = fetch_past(current, layer_at)
        tanh_part, sig_part = gating(current, earlier, conv_past[layer_at], conv_now[layer_at])
        gated_out = (tanh_part * sig_part).astype(jnp.bfloat16)
        inputs.append(current)
        earliers.append(earlier)
        saved.append((tanh_part, sig_part, gated_out))
        current = (
            current.astype(jnp.float32)
            + jnp.dot(gated_out, out_proj[layer_at], preferred_element_type=jnp.float32)
        ).astype(jnp.bfloat16)
    result = current
    upstream = cotangent
    near_list = [None] * layer_count
    for layer_at in reversed(range(layer_count)):
        current = inputs[layer_at]
        earlier = earliers[layer_at]
        tanh_part, sig_part, gated_out = saved[layer_at]
        grad_gated = jnp.dot(upstream, out_proj[layer_at].T, preferred_element_type=jnp.float32)
        grad_filter = grad_gated * sig_part * (1.0 - tanh_part * tanh_part)
        grad_gate = grad_gated * tanh_part * sig_part * (1.0 - sig_part)
        grad_preact = jnp.concatenate([grad_filter, grad_gate], 1).astype(jnp.bfloat16)
        sent_back = jnp.dot(
            grad_preact, conv_past[layer_at].T, preferred_element_type=jnp.float32
        ).astype(jnp.bfloat16)
        arrived = return_past(sent_back, layer_at)
        operands = (earlier, current, gated_out, grad_preact, upstream)
        near_list[layer_at] = near_sum(layer_term(operands, grad_scale))
        near_list, arrived = lax.optimization_barrier((near_list, arrived))
        local_grad = upstream.astype(jnp.float32) + jnp.dot(
            grad_preact, conv_now[layer_at].T, preferred_element_type=jnp.float32
        )
        upstream = (local_grad + arrived.astype(jnp.float32)).astype(jnp.bfloat16)
    first, second = far_sum(jnp.concatenate(near_list, 1))
    half_width = near_list[0].shape[1]
    summed_list = [
        jnp.concatenate(
            [
                first[:, layer_at * half_width : (layer_at + 1) * half_width],
                second[:, layer_at * half_width : (layer_at + 1) * half_width],
            ],
            1,
        )
        for layer_at in range(layer_count)
    ]
    past_list = [summed[:, :gate_width] for summed in summed_list]
    now_list = [summed[:, gate_width : 2 * gate_width] for summed in summed_list]
    out_list = [summed[:, 2 * gate_width :] for summed in summed_list]
    return (result, upstream, jnp.stack(past_list), jnp.stack(now_list), jnp.stack(out_list))


def solution(mesh):
    outer_size = mesh.shape["outer"]
    inner_size = mesh.shape["inner"]
    split = Mesh(
        mesh.devices.reshape(outer_size // 4, 2, 2, inner_size // 8, 8),
        ("y", "z_hi", "core", "x", "z_lo"),
    )
    placed = (P(EVERY, None), P(), P(), P(), P(EVERY, None))
    return jax.shard_map(
        local,
        mesh=split,
        in_specs=placed,
        out_specs=(
            P(EVERY, None),
            P(EVERY, None),
            P(None, INNER, None),
            P(None, INNER, None),
            P(None, INNER, None),
        ),
        check_vma=False,
    )
```

```python
import math

import jax
import jax.numpy as jnp
from jax import lax
from jax.sharding import Mesh
from jax.sharding import PartitionSpec as P

OUTER = ("y", "z_hi", "core")
INNER = ("x", "z_lo")
EVERY = OUTER + INNER


def group_size(axes):
    size = 1
    for axis in axes:
        size *= lax.axis_size(axis)
    return size


def group_index(axes):
    index = 0
    for axis in axes:
        index = index * lax.axis_size(axis) + lax.axis_index(axis)
    return index


def from_behind(array, axes, by):
    size = group_size(axes)
    pairs = [(i, i + by) for i in range(size) if 0 <= i + by < size]
    return lax.ppermute(array, axes, pairs)


def scatter_sum(total, axes):
    size = group_size(axes)
    own = group_index(axes)
    pieces = total.reshape(size, total.shape[0] // size, *total.shape[1:])
    summed = lax.dynamic_index_in_dim(pieces, own, 0, keepdims=False)
    for shift in range(1, size):
        piece = lax.dynamic_index_in_dim(pieces, (own + shift) % size, 0, keepdims=False)
        moved = lax.ppermute(piece.astype(jnp.bfloat16), axes, [(i, (i + shift) % size) for i in range(size)])
        summed = summed + moved.astype(jnp.float32)
    return summed


def halving_sum(total, axes):
    size = group_size(axes)
    own = group_index(axes)
    step = size // 2
    while step >= 1:
        halves = total.reshape(2, total.shape[0] // 2, *total.shape[1:])
        keep = (own // step) % 2
        kept = lax.dynamic_index_in_dim(halves, keep, 0, keepdims=False)
        given = lax.dynamic_index_in_dim(halves, 1 - keep, 0, keepdims=False)
        total = kept + lax.ppermute(given, axes, [(i, i ^ step) for i in range(size)])
        step //= 2
    return total


def everyone_sum(total, axes):
    size = group_size(axes)
    step = 1
    while step < size:
        total = total + lax.ppermute(total, axes, [(i, i ^ step) for i in range(size)])
        step *= 2
    return total


def near_sum(term):
    own_core = lax.axis_index("core")
    halves = term.reshape(term.shape[0], 2, term.shape[1] // 2)
    kept = lax.dynamic_index_in_dim(halves, own_core, 1, keepdims=False)
    given = lax.dynamic_index_in_dim(halves, 1 - own_core, 1, keepdims=False)
    moved = lax.ppermute(given.astype(jnp.bfloat16), "core", [(0, 1), (1, 0)])
    return scatter_sum(kept + moved.astype(jnp.float32), ("x",))


def far_sum(term):
    lo_size = lax.axis_size("z_lo")
    hi_size = lax.axis_size("y") * lax.axis_size("z_hi")
    rows = term.reshape(lo_size, hi_size, term.shape[1]).transpose(1, 0, 2)
    rows = rows.reshape(hi_size * lo_size, 1, term.shape[1])
    row = lax.all_to_all(rows.astype(jnp.bfloat16), ("y", "z_hi", "z_lo"), 0, 0, tiled=True)
    row = row.astype(jnp.float32).sum(0)
    spread = jnp.broadcast_to(row[None], (hi_size, *row.shape))
    term = lax.all_to_all(spread, ("y", "z_hi"), 0, 0, tiled=True).reshape(hi_size, term.shape[1])
    other = lax.ppermute(term, "core", [(0, 1), (1, 0)])
    own_core = lax.axis_index("core")
    pair = jnp.stack([term, other])
    first = lax.dynamic_index_in_dim(pair, own_core, 0, keepdims=False)
    second = lax.dynamic_index_in_dim(pair, 1 - own_core, 0, keepdims=False)
    return first, second


def gating(current, earlier, w_past, w_now):
    preact = jnp.dot(earlier, w_past, preferred_element_type=jnp.float32) + jnp.dot(
        current, w_now, preferred_element_type=jnp.float32
    )
    half_width = preact.shape[1] // 2
    return (jnp.tanh(preact[:, :half_width]), jax.nn.sigmoid(preact[:, half_width:]))


def fetch_past(series, layer_at):
    if layer_at == 0:
        return from_behind(series, EVERY, 1)
    return from_behind(series, OUTER, 2)


def return_past(series, layer_at):
    if layer_at == 0:
        return from_behind(series, EVERY, -1)
    return from_behind(series, OUTER, -2)


def layer_term(operands, grad_scale):
    earlier, current, gated_out, grad_preact, upstream = operands

    def contract(left_op, right_op):
        return lax.dot_general(
            left_op, right_op, (((0,), (0,)), ((), ())), preferred_element_type=jnp.float32
        )

    return (
        jnp.concatenate(
            [
                contract(earlier, grad_preact),
                contract(current, grad_preact),
                contract(gated_out, upstream),
            ],
            1,
        )
        * grad_scale
    )


def local(signal, conv_past, conv_now, out_proj, cotangent):
    gate_width = conv_past.shape[2]
    tick_count = signal.shape[0] * group_size(EVERY)
    grad_scale = 1.0 / math.sqrt(tick_count)
    layer_count = conv_past.shape[0]
    inputs, earliers, saved = ([], [], [])
    current = signal
    for layer_at in range(layer_count):
        earlier = fetch_past(current, layer_at)
        tanh_part, sig_part = gating(current, earlier, conv_past[layer_at], conv_now[layer_at])
        gated_out = (tanh_part * sig_part).astype(jnp.bfloat16)
        inputs.append(current)
        earliers.append(earlier)
        saved.append((tanh_part, sig_part, gated_out))
        current = (
            current.astype(jnp.float32)
            + jnp.dot(gated_out, out_proj[layer_at], preferred_element_type=jnp.float32)
        ).astype(jnp.bfloat16)
    result = current
    upstream = cotangent
    near_list = [None] * layer_count
    for layer_at in reversed(range(layer_count)):
        current = inputs[layer_at]
        earlier = earliers[layer_at]
        tanh_part, sig_part, gated_out = saved[layer_at]
        grad_gated = jnp.dot(upstream, out_proj[layer_at].T, preferred_element_type=jnp.float32)
        grad_filter = grad_gated * sig_part * (1.0 - tanh_part * tanh_part)
        grad_gate = grad_gated * tanh_part * sig_part * (1.0 - sig_part)
        grad_preact = jnp.concatenate([grad_filter, grad_gate], 1).astype(jnp.bfloat16)
        sent_back = jnp.dot(
            grad_preact, conv_past[layer_at].T, preferred_element_type=jnp.float32
        ).astype(jnp.bfloat16)
        arrived = return_past(sent_back, layer_at)
        operands = (earlier, current, gated_out, grad_preact, upstream)
        near_list[layer_at] = near_sum(layer_term(operands, grad_scale))
        if layer_at > 0:
            near_list, arrived = lax.optimization_barrier((near_list, arrived))
        local_grad = upstream.astype(jnp.float32) + jnp.dot(
            grad_preact, conv_now[layer_at].T, preferred_element_type=jnp.float32
        )
        upstream = (local_grad + arrived.astype(jnp.float32)).astype(jnp.bfloat16)
    first, second = far_sum(jnp.concatenate(near_list, 1))
    half_width = near_list[0].shape[1]
    summed_list = [
        jnp.concatenate(
            [
                first[:, layer_at * half_width : (layer_at + 1) * half_width],
                second[:, layer_at * half_width : (layer_at + 1) * half_width],
            ],
            1,
        )
        for layer_at in range(layer_count)
    ]
    past_list = [summed[:, :gate_width] for summed in summed_list]
    now_list = [summed[:, gate_width : 2 * gate_width] for summed in summed_list]
    out_list = [summed[:, 2 * gate_width :] for summed in summed_list]
    return (result, upstream, jnp.stack(past_list), jnp.stack(now_list), jnp.stack(out_list))


def solution(mesh):
    outer_size = mesh.shape["outer"]
    inner_size = mesh.shape["inner"]
    split = Mesh(
        mesh.devices.reshape(outer_size // 4, 2, 2, inner_size // 8, 8),
        ("y", "z_hi", "core", "x", "z_lo"),
    )
    placed = (P(EVERY, None), P(), P(), P(), P(EVERY, None))
    return jax.shard_map(
        local,
        mesh=split,
        in_specs=placed,
        out_specs=(
            P(EVERY, None),
            P(EVERY, None),
            P(None, INNER, None),
            P(None, INNER, None),
            P(None, INNER, None),
        ),
        check_vma=False,
    )
```

```python
import math

import jax
import jax.numpy as jnp
from jax import lax
from jax.sharding import Mesh
from jax.sharding import PartitionSpec as P

OUTER = ("y", "z_hi", "core")
INNER = ("x", "z_lo")
EVERY = OUTER + INNER


def group_size(axes):
    size = 1
    for axis in axes:
        size *= lax.axis_size(axis)
    return size


def group_index(axes):
    index = 0
    for axis in axes:
        index = index * lax.axis_size(axis) + lax.axis_index(axis)
    return index


def from_behind(array, axes, by):
    size = group_size(axes)
    pairs = [(i, i + by) for i in range(size) if 0 <= i + by < size]
    return lax.ppermute(array, axes, pairs)


def scatter_sum(total, axes):
    size = group_size(axes)
    own = group_index(axes)
    pieces = total.reshape(size, total.shape[0] // size, *total.shape[1:])
    summed = lax.dynamic_index_in_dim(pieces, own, 0, keepdims=False)
    for shift in range(1, size):
        piece = lax.dynamic_index_in_dim(pieces, (own + shift) % size, 0, keepdims=False)
        moved = lax.ppermute(piece.astype(jnp.bfloat16), axes, [(i, (i + shift) % size) for i in range(size)])
        summed = summed + moved.astype(jnp.float32)
    return summed


def halving_sum(total, axes):
    size = group_size(axes)
    own = group_index(axes)
    step = size // 2
    while step >= 1:
        halves = total.reshape(2, total.shape[0] // 2, *total.shape[1:])
        keep = (own // step) % 2
        kept = lax.dynamic_index_in_dim(halves, keep, 0, keepdims=False)
        given = lax.dynamic_index_in_dim(halves, 1 - keep, 0, keepdims=False)
        total = kept + lax.ppermute(given, axes, [(i, i ^ step) for i in range(size)])
        step //= 2
    return total


def everyone_sum(total, axes):
    size = group_size(axes)
    step = 1
    while step < size:
        total = total + lax.ppermute(total, axes, [(i, i ^ step) for i in range(size)])
        step *= 2
    return total


def near_sum(term):
    own_core = lax.axis_index("core")
    halves = term.reshape(term.shape[0], 2, term.shape[1] // 2)
    kept = lax.dynamic_index_in_dim(halves, own_core, 1, keepdims=False)
    given = lax.dynamic_index_in_dim(halves, 1 - own_core, 1, keepdims=False)
    moved = lax.ppermute(given.astype(jnp.bfloat16), "core", [(0, 1), (1, 0)])
    return scatter_sum(kept + moved.astype(jnp.float32), ("x",))


def far_sum(term):
    lo_size = lax.axis_size("z_lo")
    hi_size = lax.axis_size("y") * lax.axis_size("z_hi")
    core_size = lax.axis_size("core")
    rows = term.reshape(lo_size, hi_size, term.shape[1]).transpose(1, 0, 2)
    rows = rows.reshape(hi_size * lo_size, 1, term.shape[1])
    row = lax.all_to_all(rows.astype(jnp.bfloat16), ("y", "z_hi", "z_lo"), 0, 0, tiled=True)
    row = row.astype(jnp.float32).sum(0)
    spread = jnp.broadcast_to(row[None], (hi_size * core_size, *row.shape))
    gathered = lax.all_to_all(spread, ("y", "z_hi", "core"), 0, 0, tiled=True)
    return gathered.reshape(hi_size, core_size, term.shape[1])


def gating(current, earlier, w_past, w_now):
    preact = jnp.dot(earlier, w_past, preferred_element_type=jnp.float32) + jnp.dot(
        current, w_now, preferred_element_type=jnp.float32
    )
    half_width = preact.shape[1] // 2
    return (jnp.tanh(preact[:, :half_width]), jax.nn.sigmoid(preact[:, half_width:]))


def fetch_past(series, layer_at):
    if layer_at == 0:
        return from_behind(series, EVERY, 1)
    return from_behind(series, OUTER, 2)


def return_past(series, layer_at):
    if layer_at == 0:
        return from_behind(series, EVERY, -1)
    return from_behind(series, OUTER, -2)


def layer_term(operands, grad_scale):
    earlier, current, gated_out, grad_preact, upstream = operands

    def contract(left_op, right_op):
        return lax.dot_general(
            left_op, right_op, (((0,), (0,)), ((), ())), preferred_element_type=jnp.float32
        )

    return (
        jnp.concatenate(
            [
                contract(earlier, grad_preact),
                contract(current, grad_preact),
                contract(gated_out, upstream),
            ],
            1,
        )
        * grad_scale
    )


def local(signal, conv_past, conv_now, out_proj, cotangent):
    gate_width = conv_past.shape[2]
    tick_count = signal.shape[0] * group_size(EVERY)
    grad_scale = 1.0 / math.sqrt(tick_count)
    layer_count = conv_past.shape[0]
    inputs, earliers, saved = ([], [], [])
    current = signal
    for layer_at in range(layer_count):
        earlier = fetch_past(current, layer_at)
        tanh_part, sig_part = gating(current, earlier, conv_past[layer_at], conv_now[layer_at])
        gated_out = (tanh_part * sig_part).astype(jnp.bfloat16)
        inputs.append(current)
        earliers.append(earlier)
        saved.append((tanh_part, sig_part, gated_out))
        current = (
            current.astype(jnp.float32)
            + jnp.dot(gated_out, out_proj[layer_at], preferred_element_type=jnp.float32)
        ).astype(jnp.bfloat16)
    result = current
    upstream = cotangent
    near_list = [None] * layer_count
    for layer_at in reversed(range(layer_count)):
        current = inputs[layer_at]
        earlier = earliers[layer_at]
        tanh_part, sig_part, gated_out = saved[layer_at]
        grad_gated = jnp.dot(upstream, out_proj[layer_at].T, preferred_element_type=jnp.float32)
        grad_filter = grad_gated * sig_part * (1.0 - tanh_part * tanh_part)
        grad_gate = grad_gated * tanh_part * sig_part * (1.0 - sig_part)
        grad_preact = jnp.concatenate([grad_filter, grad_gate], 1).astype(jnp.bfloat16)
        sent_back = jnp.dot(
            grad_preact, conv_past[layer_at].T, preferred_element_type=jnp.float32
        ).astype(jnp.bfloat16)
        arrived = return_past(sent_back, layer_at)
        operands = (earlier, current, gated_out, grad_preact, upstream)
        near_list[layer_at] = near_sum(layer_term(operands, grad_scale))
        if layer_at > 0:
            near_list, arrived = lax.optimization_barrier((near_list, arrived))
        local_grad = upstream.astype(jnp.float32) + jnp.dot(
            grad_preact, conv_now[layer_at].T, preferred_element_type=jnp.float32
        )
        upstream = (local_grad + arrived.astype(jnp.float32)).astype(jnp.bfloat16)
    whole = far_sum(jnp.concatenate(near_list, 1))
    half_width = near_list[0].shape[1]
    summed_list = [
        whole[:, :, layer_at * half_width : (layer_at + 1) * half_width].reshape(
            whole.shape[0], 2 * half_width
        )
        for layer_at in range(layer_count)
    ]
    past_list = [summed[:, :gate_width] for summed in summed_list]
    now_list = [summed[:, gate_width : 2 * gate_width] for summed in summed_list]
    out_list = [summed[:, 2 * gate_width :] for summed in summed_list]
    return (result, upstream, jnp.stack(past_list), jnp.stack(now_list), jnp.stack(out_list))


def solution(mesh):
    outer_size = mesh.shape["outer"]
    inner_size = mesh.shape["inner"]
    split = Mesh(
        mesh.devices.reshape(outer_size // 4, 2, 2, inner_size // 8, 8),
        ("y", "z_hi", "core", "x", "z_lo"),
    )
    placed = (P(EVERY, None), P(), P(), P(), P(EVERY, None))
    return jax.shard_map(
        local,
        mesh=split,
        in_specs=placed,
        out_specs=(
            P(EVERY, None),
            P(EVERY, None),
            P(None, INNER, None),
            P(None, INNER, None),
            P(None, INNER, None),
        ),
        check_vma=False,
    )
```

```python
import math

import jax
import jax.numpy as jnp
from jax import lax
from jax.sharding import Mesh
from jax.sharding import PartitionSpec as P

OUTER = ("y", "z_hi", "core")
INNER = ("x", "z_lo")
EVERY = OUTER + INNER


def group_size(axes):
    size = 1
    for axis in axes:
        size *= lax.axis_size(axis)
    return size


def group_index(axes):
    index = 0
    for axis in axes:
        index = index * lax.axis_size(axis) + lax.axis_index(axis)
    return index


def from_behind(array, axes, by):
    size = group_size(axes)
    pairs = [(i, i + by) for i in range(size) if 0 <= i + by < size]
    return lax.ppermute(array, axes, pairs)


def scatter_sum(total, axes):
    size = group_size(axes)
    own = group_index(axes)
    pieces = total.reshape(size, total.shape[0] // size, *total.shape[1:])
    summed = lax.dynamic_index_in_dim(pieces, own, 0, keepdims=False)
    for shift in range(1, size):
        piece = lax.dynamic_index_in_dim(pieces, (own + shift) % size, 0, keepdims=False)
        moved = lax.ppermute(piece.astype(jnp.bfloat16), axes, [(i, (i + shift) % size) for i in range(size)])
        summed = summed + moved.astype(jnp.float32)
    return summed


def halving_sum(total, axes):
    size = group_size(axes)
    own = group_index(axes)
    step = size // 2
    while step >= 1:
        halves = total.reshape(2, total.shape[0] // 2, *total.shape[1:])
        keep = (own // step) % 2
        kept = lax.dynamic_index_in_dim(halves, keep, 0, keepdims=False)
        given = lax.dynamic_index_in_dim(halves, 1 - keep, 0, keepdims=False)
        total = kept + lax.ppermute(given, axes, [(i, i ^ step) for i in range(size)])
        step //= 2
    return total


def everyone_sum(total, axes):
    size = group_size(axes)
    step = 1
    while step < size:
        total = total + lax.ppermute(total, axes, [(i, i ^ step) for i in range(size)])
        step *= 2
    return total


def near_sum(term, by_exchange):
    own_core = lax.axis_index("core")
    halves = term.reshape(term.shape[0], 2, term.shape[1] // 2)
    kept = lax.dynamic_index_in_dim(halves, own_core, 1, keepdims=False)
    given = lax.dynamic_index_in_dim(halves, 1 - own_core, 1, keepdims=False)
    moved = lax.ppermute(given.astype(jnp.bfloat16), "core", [(0, 1), (1, 0)])
    term = kept + moved.astype(jnp.float32)
    if not by_exchange:
        return scatter_sum(term, ("x",))
    size = lax.axis_size("x")
    pieces = term.reshape(size, term.shape[0] // size, term.shape[1]).astype(jnp.bfloat16)
    return lax.all_to_all(pieces, "x", 0, 0, tiled=True).astype(jnp.float32).sum(0)


def far_sum(term):
    lo_size = lax.axis_size("z_lo")
    hi_size = lax.axis_size("y") * lax.axis_size("z_hi")
    core_size = lax.axis_size("core")
    rows = term.reshape(lo_size, hi_size, term.shape[1]).transpose(1, 0, 2)
    rows = rows.reshape(hi_size * lo_size, 1, term.shape[1])
    row = lax.all_to_all(rows.astype(jnp.bfloat16), ("y", "z_hi", "z_lo"), 0, 0, tiled=True)
    row = row.astype(jnp.float32).sum(0)
    spread = jnp.broadcast_to(row[None], (hi_size * core_size, *row.shape))
    gathered = lax.all_to_all(spread, ("y", "z_hi", "core"), 0, 0, tiled=True)
    return gathered.reshape(hi_size, core_size, term.shape[1])


def gating(current, earlier, w_past, w_now):
    preact = jnp.dot(earlier, w_past, preferred_element_type=jnp.float32) + jnp.dot(
        current, w_now, preferred_element_type=jnp.float32
    )
    half_width = preact.shape[1] // 2
    return (jnp.tanh(preact[:, :half_width]), jax.nn.sigmoid(preact[:, half_width:]))


def fetch_past(series, layer_at):
    if layer_at == 0:
        return from_behind(series, EVERY, 1)
    return from_behind(series, OUTER, 2)


def return_past(series, layer_at):
    if layer_at == 0:
        return from_behind(series, EVERY, -1)
    return from_behind(series, OUTER, -2)


def layer_term(operands, grad_scale):
    earlier, current, gated_out, grad_preact, upstream = operands

    def contract(left_op, right_op):
        return lax.dot_general(
            left_op, right_op, (((0,), (0,)), ((), ())), preferred_element_type=jnp.float32
        )

    return (
        jnp.concatenate(
            [
                contract(earlier, grad_preact),
                contract(current, grad_preact),
                contract(gated_out, upstream),
            ],
            1,
        )
        * grad_scale
    )


def local(signal, conv_past, conv_now, out_proj, cotangent):
    gate_width = conv_past.shape[2]
    tick_count = signal.shape[0] * group_size(EVERY)
    grad_scale = 1.0 / math.sqrt(tick_count)
    layer_count = conv_past.shape[0]
    inputs, earliers, saved = ([], [], [])
    current = signal
    for layer_at in range(layer_count):
        earlier = fetch_past(current, layer_at)
        tanh_part, sig_part = gating(current, earlier, conv_past[layer_at], conv_now[layer_at])
        gated_out = (tanh_part * sig_part).astype(jnp.bfloat16)
        inputs.append(current)
        earliers.append(earlier)
        saved.append((tanh_part, sig_part, gated_out))
        current = (
            current.astype(jnp.float32)
            + jnp.dot(gated_out, out_proj[layer_at], preferred_element_type=jnp.float32)
        ).astype(jnp.bfloat16)
    result = current
    upstream = cotangent
    near_list = [None] * layer_count
    for layer_at in reversed(range(layer_count)):
        current = inputs[layer_at]
        earlier = earliers[layer_at]
        tanh_part, sig_part, gated_out = saved[layer_at]
        grad_gated = jnp.dot(upstream, out_proj[layer_at].T, preferred_element_type=jnp.float32)
        grad_filter = grad_gated * sig_part * (1.0 - tanh_part * tanh_part)
        grad_gate = grad_gated * tanh_part * sig_part * (1.0 - sig_part)
        grad_preact = jnp.concatenate([grad_filter, grad_gate], 1).astype(jnp.bfloat16)
        sent_back = jnp.dot(
            grad_preact, conv_past[layer_at].T, preferred_element_type=jnp.float32
        ).astype(jnp.bfloat16)
        arrived = return_past(sent_back, layer_at)
        operands = (earlier, current, gated_out, grad_preact, upstream)
        near_list[layer_at] = near_sum(layer_term(operands, grad_scale), layer_at == 0)
        if layer_at > 0:
            near_list, arrived = lax.optimization_barrier((near_list, arrived))
        local_grad = upstream.astype(jnp.float32) + jnp.dot(
            grad_preact, conv_now[layer_at].T, preferred_element_type=jnp.float32
        )
        upstream = (local_grad + arrived.astype(jnp.float32)).astype(jnp.bfloat16)
    whole = far_sum(jnp.concatenate(near_list, 1))
    half_width = near_list[0].shape[1]
    summed_list = [
        whole[:, :, layer_at * half_width : (layer_at + 1) * half_width].reshape(
            whole.shape[0], 2 * half_width
        )
        for layer_at in range(layer_count)
    ]
    past_list = [summed[:, :gate_width] for summed in summed_list]
    now_list = [summed[:, gate_width : 2 * gate_width] for summed in summed_list]
    out_list = [summed[:, 2 * gate_width :] for summed in summed_list]
    return (result, upstream, jnp.stack(past_list), jnp.stack(now_list), jnp.stack(out_list))


def solution(mesh):
    outer_size = mesh.shape["outer"]
    inner_size = mesh.shape["inner"]
    split = Mesh(
        mesh.devices.reshape(outer_size // 4, 2, 2, inner_size // 8, 8),
        ("y", "z_hi", "core", "x", "z_lo"),
    )
    placed = (P(EVERY, None), P(), P(), P(), P(EVERY, None))
    return jax.shard_map(
        local,
        mesh=split,
        in_specs=placed,
        out_specs=(
            P(EVERY, None),
            P(EVERY, None),
            P(None, INNER, None),
            P(None, INNER, None),
            P(None, INNER, None),
        ),
        check_vma=False,
    )
```

```python
import math

import jax
import jax.numpy as jnp
from jax import lax
from jax.sharding import Mesh
from jax.sharding import PartitionSpec as P

OUTER = ("y", "z_hi", "core")
INNER = ("x", "z_lo")
EVERY = OUTER + INNER


def group_size(axes):
    size = 1
    for axis in axes:
        size *= lax.axis_size(axis)
    return size


def group_index(axes):
    index = 0
    for axis in axes:
        index = index * lax.axis_size(axis) + lax.axis_index(axis)
    return index


def from_behind(array, axes, by):
    size = group_size(axes)
    pairs = [(i, i + by) for i in range(size) if 0 <= i + by < size]
    return lax.ppermute(array, axes, pairs)


def scatter_sum(total, axes):
    size = group_size(axes)
    own = group_index(axes)
    pieces = total.reshape(size, total.shape[0] // size, *total.shape[1:])
    summed = lax.dynamic_index_in_dim(pieces, own, 0, keepdims=False)
    for shift in range(1, size):
        piece = lax.dynamic_index_in_dim(pieces, (own + shift) % size, 0, keepdims=False)
        moved = lax.ppermute(piece.astype(jnp.bfloat16), axes, [(i, (i + shift) % size) for i in range(size)])
        summed = summed + moved.astype(jnp.float32)
    return summed


def halving_sum(total, axes):
    size = group_size(axes)
    own = group_index(axes)
    step = size // 2
    while step >= 1:
        halves = total.reshape(2, total.shape[0] // 2, *total.shape[1:])
        keep = (own // step) % 2
        kept = lax.dynamic_index_in_dim(halves, keep, 0, keepdims=False)
        given = lax.dynamic_index_in_dim(halves, 1 - keep, 0, keepdims=False)
        total = kept + lax.ppermute(given, axes, [(i, i ^ step) for i in range(size)])
        step //= 2
    return total


def everyone_sum(total, axes):
    size = group_size(axes)
    step = 1
    while step < size:
        total = total + lax.ppermute(total, axes, [(i, i ^ step) for i in range(size)])
        step *= 2
    return total


def near_sum(term):
    own_core = lax.axis_index("core")
    halves = term.reshape(term.shape[0], 2, term.shape[1] // 2)
    kept = lax.dynamic_index_in_dim(halves, own_core, 1, keepdims=False)
    given = lax.dynamic_index_in_dim(halves, 1 - own_core, 1, keepdims=False)
    moved = lax.ppermute(given.astype(jnp.bfloat16), "core", [(0, 1), (1, 0)])
    return kept + moved.astype(jnp.float32)


def far_sum(term):
    x_size = lax.axis_size("x")
    lo_size = lax.axis_size("z_lo")
    hi_size = lax.axis_size("y") * lax.axis_size("z_hi")
    core_size = lax.axis_size("core")
    rows = term.reshape(x_size, lo_size, hi_size, term.shape[1]).transpose(2, 0, 1, 3)
    rows = rows.reshape(hi_size * x_size * lo_size, 1, term.shape[1])
    row = lax.all_to_all(rows.astype(jnp.bfloat16), ("y", "z_hi", "x", "z_lo"), 0, 0, tiled=True)
    row = row.astype(jnp.float32).sum(0)
    spread = jnp.broadcast_to(row[None], (hi_size * core_size, *row.shape))
    gathered = lax.all_to_all(spread, ("y", "z_hi", "core"), 0, 0, tiled=True)
    return gathered.reshape(hi_size, core_size, term.shape[1])


def gating(current, earlier, w_past, w_now):
    preact = jnp.dot(earlier, w_past, preferred_element_type=jnp.float32) + jnp.dot(
        current, w_now, preferred_element_type=jnp.float32
    )
    half_width = preact.shape[1] // 2
    return (jnp.tanh(preact[:, :half_width]), jax.nn.sigmoid(preact[:, half_width:]))


def fetch_past(series, layer_at):
    if layer_at == 0:
        return from_behind(series, EVERY, 1)
    return from_behind(series, OUTER, 2)


def return_past(series, layer_at):
    if layer_at == 0:
        return from_behind(series, EVERY, -1)
    return from_behind(series, OUTER, -2)


def layer_term(operands, grad_scale):
    earlier, current, gated_out, grad_preact, upstream = operands

    def contract(left_op, right_op):
        return lax.dot_general(
            left_op, right_op, (((0,), (0,)), ((), ())), preferred_element_type=jnp.float32
        )

    return (
        jnp.concatenate(
            [
                contract(earlier, grad_preact),
                contract(current, grad_preact),
                contract(gated_out, upstream),
            ],
            1,
        )
        * grad_scale
    )


def local(signal, conv_past, conv_now, out_proj, cotangent):
    gate_width = conv_past.shape[2]
    tick_count = signal.shape[0] * group_size(EVERY)
    grad_scale = 1.0 / math.sqrt(tick_count)
    layer_count = conv_past.shape[0]
    inputs, earliers, saved = ([], [], [])
    current = signal
    for layer_at in range(layer_count):
        earlier = fetch_past(current, layer_at)
        tanh_part, sig_part = gating(current, earlier, conv_past[layer_at], conv_now[layer_at])
        gated_out = (tanh_part * sig_part).astype(jnp.bfloat16)
        inputs.append(current)
        earliers.append(earlier)
        saved.append((tanh_part, sig_part, gated_out))
        current = (
            current.astype(jnp.float32)
            + jnp.dot(gated_out, out_proj[layer_at], preferred_element_type=jnp.float32)
        ).astype(jnp.bfloat16)
    result = current
    upstream = cotangent
    near_list = [None] * layer_count
    for layer_at in reversed(range(layer_count)):
        current = inputs[layer_at]
        earlier = earliers[layer_at]
        tanh_part, sig_part, gated_out = saved[layer_at]
        grad_gated = jnp.dot(upstream, out_proj[layer_at].T, preferred_element_type=jnp.float32)
        grad_filter = grad_gated * sig_part * (1.0 - tanh_part * tanh_part)
        grad_gate = grad_gated * tanh_part * sig_part * (1.0 - sig_part)
        grad_preact = jnp.concatenate([grad_filter, grad_gate], 1).astype(jnp.bfloat16)
        sent_back = jnp.dot(
            grad_preact, conv_past[layer_at].T, preferred_element_type=jnp.float32
        ).astype(jnp.bfloat16)
        arrived = return_past(sent_back, layer_at)
        operands = (earlier, current, gated_out, grad_preact, upstream)
        near_list[layer_at] = near_sum(layer_term(operands, grad_scale))
        if layer_at > 0:
            near_list, arrived = lax.optimization_barrier((near_list, arrived))
        local_grad = upstream.astype(jnp.float32) + jnp.dot(
            grad_preact, conv_now[layer_at].T, preferred_element_type=jnp.float32
        )
        upstream = (local_grad + arrived.astype(jnp.float32)).astype(jnp.bfloat16)
    whole = far_sum(jnp.concatenate(near_list, 1))
    half_width = near_list[0].shape[1]
    summed_list = [
        whole[:, :, layer_at * half_width : (layer_at + 1) * half_width].reshape(
            whole.shape[0], 2 * half_width
        )
        for layer_at in range(layer_count)
    ]
    past_list = [summed[:, :gate_width] for summed in summed_list]
    now_list = [summed[:, gate_width : 2 * gate_width] for summed in summed_list]
    out_list = [summed[:, 2 * gate_width :] for summed in summed_list]
    return (result, upstream, jnp.stack(past_list), jnp.stack(now_list), jnp.stack(out_list))


def solution(mesh):
    outer_size = mesh.shape["outer"]
    inner_size = mesh.shape["inner"]
    split = Mesh(
        mesh.devices.reshape(outer_size // 4, 2, 2, inner_size // 8, 8),
        ("y", "z_hi", "core", "x", "z_lo"),
    )
    placed = (P(EVERY, None), P(), P(), P(), P(EVERY, None))
    return jax.shard_map(
        local,
        mesh=split,
        in_specs=placed,
        out_specs=(
            P(EVERY, None),
            P(EVERY, None),
            P(None, INNER, None),
            P(None, INNER, None),
            P(None, INNER, None),
        ),
        check_vma=False,
    )
```

```python
import math

import jax
import jax.numpy as jnp
from jax import lax
from jax.sharding import Mesh
from jax.sharding import PartitionSpec as P

OUTER = ("y", "z_hi", "core")
INNER = ("x", "z_lo")
EVERY = OUTER + INNER


def group_size(axes):
    size = 1
    for axis in axes:
        size *= lax.axis_size(axis)
    return size


def group_index(axes):
    index = 0
    for axis in axes:
        index = index * lax.axis_size(axis) + lax.axis_index(axis)
    return index


def from_behind(array, axes, by):
    size = group_size(axes)
    pairs = [(i, i + by) for i in range(size) if 0 <= i + by < size]
    return lax.ppermute(array, axes, pairs)


def scatter_sum(total, axes):
    size = group_size(axes)
    own = group_index(axes)
    pieces = total.reshape(size, total.shape[0] // size, *total.shape[1:])
    summed = lax.dynamic_index_in_dim(pieces, own, 0, keepdims=False)
    for shift in range(1, size):
        piece = lax.dynamic_index_in_dim(pieces, (own + shift) % size, 0, keepdims=False)
        moved = lax.ppermute(piece.astype(jnp.bfloat16), axes, [(i, (i + shift) % size) for i in range(size)])
        summed = summed + moved.astype(jnp.float32)
    return summed


def halving_sum(total, axes):
    size = group_size(axes)
    own = group_index(axes)
    step = size // 2
    while step >= 1:
        halves = total.reshape(2, total.shape[0] // 2, *total.shape[1:])
        keep = (own // step) % 2
        kept = lax.dynamic_index_in_dim(halves, keep, 0, keepdims=False)
        given = lax.dynamic_index_in_dim(halves, 1 - keep, 0, keepdims=False)
        total = kept + lax.ppermute(given, axes, [(i, i ^ step) for i in range(size)])
        step //= 2
    return total


def everyone_sum(total, axes):
    size = group_size(axes)
    step = 1
    while step < size:
        total = total + lax.ppermute(total, axes, [(i, i ^ step) for i in range(size)])
        step *= 2
    return total


def near_sum(term, by_exchange):
    own_core = lax.axis_index("core")
    halves = term.reshape(term.shape[0], 2, term.shape[1] // 2)
    kept = lax.dynamic_index_in_dim(halves, own_core, 1, keepdims=False)
    given = lax.dynamic_index_in_dim(halves, 1 - own_core, 1, keepdims=False)
    moved = lax.ppermute(given.astype(jnp.bfloat16), "core", [(0, 1), (1, 0)])
    term = kept + moved.astype(jnp.float32)
    if not by_exchange:
        return scatter_sum(term, ("x",))
    size = lax.axis_size("x")
    pieces = term.reshape(size, term.shape[0] // size, term.shape[1]).astype(jnp.bfloat16)
    return lax.all_to_all(pieces, "x", 0, 0, tiled=True).astype(jnp.float32).sum(0)


def far_sum(term):
    lo_size = lax.axis_size("z_lo")
    hi_size = lax.axis_size("y") * lax.axis_size("z_hi")
    core_size = lax.axis_size("core")
    rows = term.reshape(lo_size, hi_size, term.shape[1]).transpose(1, 0, 2)
    rows = rows.reshape(hi_size * lo_size, 1, term.shape[1])
    row = lax.all_to_all(rows.astype(jnp.bfloat16), ("y", "z_hi", "z_lo"), 0, 0, tiled=True)
    row = row.astype(jnp.float32).sum(0)
    spread = jnp.broadcast_to(row[None], (hi_size * core_size, *row.shape))
    gathered = lax.all_to_all(spread, ("y", "z_hi", "core"), 0, 0, tiled=True)
    return gathered.reshape(hi_size, core_size, term.shape[1])


def gating(current, earlier, w_past, w_now):
    preact = jnp.dot(earlier, w_past, preferred_element_type=jnp.float32) + jnp.dot(
        current, w_now, preferred_element_type=jnp.float32
    )
    half_width = preact.shape[1] // 2
    return (jnp.tanh(preact[:, :half_width]), jax.nn.sigmoid(preact[:, half_width:]))


def fetch_past(series, layer_at):
    if layer_at == 0:
        return from_behind(series, EVERY, 1)
    return from_behind(series, OUTER, 2)


def return_past(series, layer_at):
    if layer_at == 0:
        return from_behind(series, EVERY, -1)
    return from_behind(series, OUTER, -2)


def layer_term(operands, grad_scale):
    earlier, current, gated_out, grad_preact, upstream = operands

    def contract(left_op, right_op):
        return lax.dot_general(
            left_op, right_op, (((0,), (0,)), ((), ())), preferred_element_type=jnp.float32
        )

    return (
        jnp.concatenate(
            [
                contract(earlier, grad_preact),
                contract(current, grad_preact),
                contract(gated_out, upstream),
            ],
            1,
        )
        * grad_scale
    )


def local(signal, conv_past, conv_now, out_proj, cotangent):
    gate_width = conv_past.shape[2]
    tick_count = signal.shape[0] * group_size(EVERY)
    grad_scale = 1.0 / math.sqrt(tick_count)
    layer_count = conv_past.shape[0]
    inputs, earliers, saved = ([], [], [])
    current = signal
    for layer_at in range(layer_count):
        earlier = fetch_past(current, layer_at)
        tanh_part, sig_part = gating(current, earlier, conv_past[layer_at], conv_now[layer_at])
        gated_out = (tanh_part * sig_part).astype(jnp.bfloat16)
        inputs.append(current)
        earliers.append(earlier)
        saved.append((tanh_part, sig_part, gated_out))
        current = (
            current.astype(jnp.float32)
            + jnp.dot(gated_out, out_proj[layer_at], preferred_element_type=jnp.float32)
        ).astype(jnp.bfloat16)
    result = current
    upstream = cotangent
    near_list = [None] * layer_count
    for layer_at in reversed(range(layer_count)):
        current = inputs[layer_at]
        earlier = earliers[layer_at]
        tanh_part, sig_part, gated_out = saved[layer_at]
        grad_gated = jnp.dot(upstream, out_proj[layer_at].T, preferred_element_type=jnp.float32)
        grad_filter = grad_gated * sig_part * (1.0 - tanh_part * tanh_part)
        grad_gate = grad_gated * tanh_part * sig_part * (1.0 - sig_part)
        grad_preact = jnp.concatenate([grad_filter, grad_gate], 1).astype(jnp.bfloat16)
        sent_back = jnp.dot(
            grad_preact, conv_past[layer_at].T, preferred_element_type=jnp.float32
        ).astype(jnp.bfloat16)
        grad_preact, sent_back = lax.optimization_barrier((grad_preact, sent_back))
        arrived = return_past(sent_back, layer_at)
        operands = (earlier, current, gated_out, grad_preact, upstream)
        near_list[layer_at] = near_sum(layer_term(operands, grad_scale), layer_at == 0)
        if layer_at > 0:
            near_list, arrived = lax.optimization_barrier((near_list, arrived))
        local_grad = upstream.astype(jnp.float32) + jnp.dot(
            grad_preact, conv_now[layer_at].T, preferred_element_type=jnp.float32
        )
        upstream = (local_grad + arrived.astype(jnp.float32)).astype(jnp.bfloat16)
    whole = far_sum(jnp.concatenate(near_list, 1))
    half_width = near_list[0].shape[1]
    summed_list = [
        whole[:, :, layer_at * half_width : (layer_at + 1) * half_width].reshape(
            whole.shape[0], 2 * half_width
        )
        for layer_at in range(layer_count)
    ]
    past_list = [summed[:, :gate_width] for summed in summed_list]
    now_list = [summed[:, gate_width : 2 * gate_width] for summed in summed_list]
    out_list = [summed[:, 2 * gate_width :] for summed in summed_list]
    return (result, upstream, jnp.stack(past_list), jnp.stack(now_list), jnp.stack(out_list))


def solution(mesh):
    outer_size = mesh.shape["outer"]
    inner_size = mesh.shape["inner"]
    split = Mesh(
        mesh.devices.reshape(outer_size // 4, 2, 2, inner_size // 8, 8),
        ("y", "z_hi", "core", "x", "z_lo"),
    )
    placed = (P(EVERY, None), P(), P(), P(), P(EVERY, None))
    return jax.shard_map(
        local,
        mesh=split,
        in_specs=placed,
        out_specs=(
            P(EVERY, None),
            P(EVERY, None),
            P(None, INNER, None),
            P(None, INNER, None),
            P(None, INNER, None),
        ),
        check_vma=False,
    )
```

```python
import math

import jax
import jax.numpy as jnp
from jax import lax
from jax.sharding import Mesh
from jax.sharding import PartitionSpec as P

OUTER = ("y", "z_hi", "core")
INNER = ("x", "z_lo")
EVERY = OUTER + INNER


def group_size(axes):
    size = 1
    for axis in axes:
        size *= lax.axis_size(axis)
    return size


def group_index(axes):
    index = 0
    for axis in axes:
        index = index * lax.axis_size(axis) + lax.axis_index(axis)
    return index


def from_behind(array, axes, by):
    size = group_size(axes)
    pairs = [(i, i + by) for i in range(size) if 0 <= i + by < size]
    return lax.ppermute(array, axes, pairs)


def scatter_sum(total, axes):
    size = group_size(axes)
    own = group_index(axes)
    pieces = total.reshape(size, total.shape[0] // size, *total.shape[1:])
    summed = lax.dynamic_index_in_dim(pieces, own, 0, keepdims=False)
    for shift in range(1, size):
        piece = lax.dynamic_index_in_dim(pieces, (own + shift) % size, 0, keepdims=False)
        moved = lax.ppermute(piece.astype(jnp.bfloat16), axes, [(i, (i + shift) % size) for i in range(size)])
        summed = summed + moved.astype(jnp.float32)
    return summed


def halving_sum(total, axes):
    size = group_size(axes)
    own = group_index(axes)
    step = size // 2
    while step >= 1:
        halves = total.reshape(2, total.shape[0] // 2, *total.shape[1:])
        keep = (own // step) % 2
        kept = lax.dynamic_index_in_dim(halves, keep, 0, keepdims=False)
        given = lax.dynamic_index_in_dim(halves, 1 - keep, 0, keepdims=False)
        total = kept + lax.ppermute(given, axes, [(i, i ^ step) for i in range(size)])
        step //= 2
    return total


def everyone_sum(total, axes):
    size = group_size(axes)
    step = 1
    while step < size:
        total = total + lax.ppermute(total, axes, [(i, i ^ step) for i in range(size)])
        step *= 2
    return total


def near_sum(term, by_exchange):
    if by_exchange:
        core_size = lax.axis_size("core")
        x_size = lax.axis_size("x")
        pieces = term.reshape(x_size, term.shape[0] // x_size, core_size, term.shape[1] // core_size)
        pieces = pieces.transpose(2, 0, 1, 3).reshape(core_size * x_size, term.shape[0] // x_size, -1)
        moved = lax.all_to_all(pieces.astype(jnp.bfloat16), ("core", "x"), 0, 0, tiled=True)
        return moved.astype(jnp.float32).sum(0)
    own_core = lax.axis_index("core")
    halves = term.reshape(term.shape[0], 2, term.shape[1] // 2)
    kept = lax.dynamic_index_in_dim(halves, own_core, 1, keepdims=False)
    given = lax.dynamic_index_in_dim(halves, 1 - own_core, 1, keepdims=False)
    moved = lax.ppermute(given.astype(jnp.bfloat16), "core", [(0, 1), (1, 0)])
    return scatter_sum(kept + moved.astype(jnp.float32), ("x",))


def far_sum(term):
    lo_size = lax.axis_size("z_lo")
    hi_size = lax.axis_size("y") * lax.axis_size("z_hi")
    core_size = lax.axis_size("core")
    rows = term.reshape(lo_size, hi_size, term.shape[1]).transpose(1, 0, 2)
    rows = rows.reshape(hi_size * lo_size, 1, term.shape[1])
    row = lax.all_to_all(rows.astype(jnp.bfloat16), ("y", "z_hi", "z_lo"), 0, 0, tiled=True)
    row = row.astype(jnp.float32).sum(0)
    spread = jnp.broadcast_to(row[None], (hi_size * core_size, *row.shape))
    gathered = lax.all_to_all(spread, ("y", "z_hi", "core"), 0, 0, tiled=True)
    return gathered.reshape(hi_size, core_size, term.shape[1])


def gating(current, earlier, w_past, w_now):
    preact = jnp.dot(earlier, w_past, preferred_element_type=jnp.float32) + jnp.dot(
        current, w_now, preferred_element_type=jnp.float32
    )
    half_width = preact.shape[1] // 2
    return (jnp.tanh(preact[:, :half_width]), jax.nn.sigmoid(preact[:, half_width:]))


def fetch_past(series, layer_at):
    if layer_at == 0:
        return from_behind(series, EVERY, 1)
    return from_behind(series, OUTER, 2)


def return_past(series, layer_at):
    if layer_at == 0:
        return from_behind(series, EVERY, -1)
    return from_behind(series, OUTER, -2)


def layer_term(operands, grad_scale):
    earlier, current, gated_out, grad_preact, upstream = operands

    def contract(left_op, right_op):
        return lax.dot_general(
            left_op, right_op, (((0,), (0,)), ((), ())), preferred_element_type=jnp.float32
        )

    return (
        jnp.concatenate(
            [
                contract(earlier, grad_preact),
                contract(current, grad_preact),
                contract(gated_out, upstream),
            ],
            1,
        )
        * grad_scale
    )


def local(signal, conv_past, conv_now, out_proj, cotangent):
    gate_width = conv_past.shape[2]
    tick_count = signal.shape[0] * group_size(EVERY)
    grad_scale = 1.0 / math.sqrt(tick_count)
    layer_count = conv_past.shape[0]
    inputs, earliers, saved = ([], [], [])
    current = signal
    for layer_at in range(layer_count):
        earlier = fetch_past(current, layer_at)
        tanh_part, sig_part = gating(current, earlier, conv_past[layer_at], conv_now[layer_at])
        gated_out = (tanh_part * sig_part).astype(jnp.bfloat16)
        inputs.append(current)
        earliers.append(earlier)
        saved.append((tanh_part, sig_part, gated_out))
        current = (
            current.astype(jnp.float32)
            + jnp.dot(gated_out, out_proj[layer_at], preferred_element_type=jnp.float32)
        ).astype(jnp.bfloat16)
    result = current
    upstream = cotangent
    near_list = [None] * layer_count
    for layer_at in reversed(range(layer_count)):
        current = inputs[layer_at]
        earlier = earliers[layer_at]
        tanh_part, sig_part, gated_out = saved[layer_at]
        grad_gated = jnp.dot(upstream, out_proj[layer_at].T, preferred_element_type=jnp.float32)
        grad_filter = grad_gated * sig_part * (1.0 - tanh_part * tanh_part)
        grad_gate = grad_gated * tanh_part * sig_part * (1.0 - sig_part)
        grad_preact = jnp.concatenate([grad_filter, grad_gate], 1).astype(jnp.bfloat16)
        sent_back = jnp.dot(
            grad_preact, conv_past[layer_at].T, preferred_element_type=jnp.float32
        ).astype(jnp.bfloat16)
        arrived = return_past(sent_back, layer_at)
        operands = (earlier, current, gated_out, grad_preact, upstream)
        near_list[layer_at] = near_sum(layer_term(operands, grad_scale), layer_at == 0)
        if layer_at > 0:
            near_list, arrived = lax.optimization_barrier((near_list, arrived))
        local_grad = upstream.astype(jnp.float32) + jnp.dot(
            grad_preact, conv_now[layer_at].T, preferred_element_type=jnp.float32
        )
        upstream = (local_grad + arrived.astype(jnp.float32)).astype(jnp.bfloat16)
    whole = far_sum(jnp.concatenate(near_list, 1))
    half_width = near_list[0].shape[1]
    summed_list = [
        whole[:, :, layer_at * half_width : (layer_at + 1) * half_width].reshape(
            whole.shape[0], 2 * half_width
        )
        for layer_at in range(layer_count)
    ]
    past_list = [summed[:, :gate_width] for summed in summed_list]
    now_list = [summed[:, gate_width : 2 * gate_width] for summed in summed_list]
    out_list = [summed[:, 2 * gate_width :] for summed in summed_list]
    return (result, upstream, jnp.stack(past_list), jnp.stack(now_list), jnp.stack(out_list))


def solution(mesh):
    outer_size = mesh.shape["outer"]
    inner_size = mesh.shape["inner"]
    split = Mesh(
        mesh.devices.reshape(outer_size // 4, 2, 2, inner_size // 8, 8),
        ("y", "z_hi", "core", "x", "z_lo"),
    )
    placed = (P(EVERY, None), P(), P(), P(), P(EVERY, None))
    return jax.shard_map(
        local,
        mesh=split,
        in_specs=placed,
        out_specs=(
            P(EVERY, None),
            P(EVERY, None),
            P(None, INNER, None),
            P(None, INNER, None),
            P(None, INNER, None),
        ),
        check_vma=False,
    )
```

```python
import math

import jax
import jax.numpy as jnp
from jax import lax
from jax.sharding import Mesh
from jax.sharding import PartitionSpec as P

OUTER = ("y", "z_hi", "core")
INNER = ("x", "z_lo")
EVERY = OUTER + INNER


def group_size(axes):
    size = 1
    for axis in axes:
        size *= lax.axis_size(axis)
    return size


def group_index(axes):
    index = 0
    for axis in axes:
        index = index * lax.axis_size(axis) + lax.axis_index(axis)
    return index


def from_behind(array, axes, by):
    size = group_size(axes)
    pairs = [(i, i + by) for i in range(size) if 0 <= i + by < size]
    return lax.ppermute(array, axes, pairs)


def scatter_sum(total, axes):
    size = group_size(axes)
    own = group_index(axes)
    pieces = total.reshape(size, total.shape[0] // size, *total.shape[1:])
    summed = lax.dynamic_index_in_dim(pieces, own, 0, keepdims=False)
    for shift in range(1, size):
        piece = lax.dynamic_index_in_dim(pieces, (own + shift) % size, 0, keepdims=False)
        moved = lax.ppermute(piece.astype(jnp.bfloat16), axes, [(i, (i + shift) % size) for i in range(size)])
        summed = summed + moved.astype(jnp.float32)
    return summed


def halving_sum(total, axes):
    size = group_size(axes)
    own = group_index(axes)
    step = size // 2
    while step >= 1:
        halves = total.reshape(2, total.shape[0] // 2, *total.shape[1:])
        keep = (own // step) % 2
        kept = lax.dynamic_index_in_dim(halves, keep, 0, keepdims=False)
        given = lax.dynamic_index_in_dim(halves, 1 - keep, 0, keepdims=False)
        total = kept + lax.ppermute(given, axes, [(i, i ^ step) for i in range(size)])
        step //= 2
    return total


def everyone_sum(total, axes):
    size = group_size(axes)
    step = 1
    while step < size:
        total = total + lax.ppermute(total, axes, [(i, i ^ step) for i in range(size)])
        step *= 2
    return total


def near_sum(term, by_exchange):
    own_core = lax.axis_index("core")
    halves = term.reshape(term.shape[0], 2, term.shape[1] // 2)
    kept = lax.dynamic_index_in_dim(halves, own_core, 1, keepdims=False)
    given = lax.dynamic_index_in_dim(halves, 1 - own_core, 1, keepdims=False)
    moved = lax.ppermute(given.astype(jnp.bfloat16), "core", [(0, 1), (1, 0)])
    term = kept + moved.astype(jnp.float32)
    if not by_exchange:
        return scatter_sum(term, ("x",))
    size = lax.axis_size("x")
    pieces = term.reshape(size, term.shape[0] // size, term.shape[1]).astype(jnp.bfloat16)
    return lax.all_to_all(pieces, "x", 0, 0, tiled=True).astype(jnp.float32).sum(0)


def far_sum(term):
    lo_size = lax.axis_size("z_lo")
    hi_size = lax.axis_size("y") * lax.axis_size("z_hi")
    core_size = lax.axis_size("core")
    rows = term.reshape(lo_size, hi_size, term.shape[1]).transpose(1, 0, 2)
    rows = rows.reshape(hi_size * lo_size, 1, term.shape[1])
    row = lax.all_to_all(rows, ("y", "z_hi", "z_lo"), 0, 0, tiled=True).sum(0)
    spread = jnp.broadcast_to(row[None], (hi_size * core_size, *row.shape))
    gathered = lax.all_to_all(spread, ("y", "z_hi", "core"), 0, 0, tiled=True)
    return gathered.reshape(hi_size, core_size, term.shape[1])


def gating(current, earlier, w_past, w_now):
    preact = jnp.dot(earlier, w_past, preferred_element_type=jnp.float32) + jnp.dot(
        current, w_now, preferred_element_type=jnp.float32
    )
    half_width = preact.shape[1] // 2
    return (jnp.tanh(preact[:, :half_width]), jax.nn.sigmoid(preact[:, half_width:]))


def fetch_past(series, layer_at):
    if layer_at == 0:
        return from_behind(series, EVERY, 1)
    return from_behind(series, OUTER, 2)


def return_past(series, layer_at):
    if layer_at == 0:
        return from_behind(series, EVERY, -1)
    return from_behind(series, OUTER, -2)


def layer_term(operands, grad_scale):
    earlier, current, gated_out, grad_preact, upstream = operands

    def contract(left_op, right_op):
        return lax.dot_general(
            left_op, right_op, (((0,), (0,)), ((), ())), preferred_element_type=jnp.float32
        )

    return (
        jnp.concatenate(
            [
                contract(earlier, grad_preact),
                contract(current, grad_preact),
                contract(gated_out, upstream),
            ],
            1,
        )
        * grad_scale
    )


def local(signal, conv_past, conv_now, out_proj, cotangent):
    gate_width = conv_past.shape[2]
    tick_count = signal.shape[0] * group_size(EVERY)
    grad_scale = 1.0 / math.sqrt(tick_count)
    layer_count = conv_past.shape[0]
    inputs, earliers, saved = ([], [], [])
    current = signal
    for layer_at in range(layer_count):
        earlier = fetch_past(current, layer_at)
        tanh_part, sig_part = gating(current, earlier, conv_past[layer_at], conv_now[layer_at])
        gated_out = (tanh_part * sig_part).astype(jnp.bfloat16)
        inputs.append(current)
        earliers.append(earlier)
        saved.append((tanh_part, sig_part, gated_out))
        current = (
            current.astype(jnp.float32)
            + jnp.dot(gated_out, out_proj[layer_at], preferred_element_type=jnp.float32)
        ).astype(jnp.bfloat16)
    result = current
    upstream = cotangent
    near_list = [None] * layer_count
    for layer_at in reversed(range(layer_count)):
        current = inputs[layer_at]
        earlier = earliers[layer_at]
        tanh_part, sig_part, gated_out = saved[layer_at]
        grad_gated = jnp.dot(upstream, out_proj[layer_at].T, preferred_element_type=jnp.float32)
        grad_filter = grad_gated * sig_part * (1.0 - tanh_part * tanh_part)
        grad_gate = grad_gated * tanh_part * sig_part * (1.0 - sig_part)
        grad_preact = jnp.concatenate([grad_filter, grad_gate], 1).astype(jnp.bfloat16)
        sent_back = jnp.dot(
            grad_preact, conv_past[layer_at].T, preferred_element_type=jnp.float32
        ).astype(jnp.bfloat16)
        arrived = return_past(sent_back, layer_at)
        operands = (earlier, current, gated_out, grad_preact, upstream)
        near_list[layer_at] = near_sum(layer_term(operands, grad_scale), layer_at == 0)
        if layer_at > 0:
            near_list, arrived = lax.optimization_barrier((near_list, arrived))
        local_grad = upstream.astype(jnp.float32) + jnp.dot(
            grad_preact, conv_now[layer_at].T, preferred_element_type=jnp.float32
        )
        upstream = (local_grad + arrived.astype(jnp.float32)).astype(jnp.bfloat16)
    whole = far_sum(jnp.concatenate(near_list, 1))
    half_width = near_list[0].shape[1]
    summed_list = [
        whole[:, :, layer_at * half_width : (layer_at + 1) * half_width].reshape(
            whole.shape[0], 2 * half_width
        )
        for layer_at in range(layer_count)
    ]
    past_list = [summed[:, :gate_width] for summed in summed_list]
    now_list = [summed[:, gate_width : 2 * gate_width] for summed in summed_list]
    out_list = [summed[:, 2 * gate_width :] for summed in summed_list]
    return (result, upstream, jnp.stack(past_list), jnp.stack(now_list), jnp.stack(out_list))


def solution(mesh):
    outer_size = mesh.shape["outer"]
    inner_size = mesh.shape["inner"]
    split = Mesh(
        mesh.devices.reshape(outer_size // 4, 2, 2, inner_size // 8, 8),
        ("y", "z_hi", "core", "x", "z_lo"),
    )
    placed = (P(EVERY, None), P(), P(), P(), P(EVERY, None))
    return jax.shard_map(
        local,
        mesh=split,
        in_specs=placed,
        out_specs=(
            P(EVERY, None),
            P(EVERY, None),
            P(None, INNER, None),
            P(None, INNER, None),
            P(None, INNER, None),
        ),
        check_vma=False,
    )
```

```python
import math

import jax
import jax.numpy as jnp
from jax import lax
from jax.sharding import Mesh
from jax.sharding import PartitionSpec as P

OUTER = ("y", "z_hi", "core")
INNER = ("x", "z_lo")
EVERY = OUTER + INNER


def group_size(axes):
    size = 1
    for axis in axes:
        size *= lax.axis_size(axis)
    return size


def group_index(axes):
    index = 0
    for axis in axes:
        index = index * lax.axis_size(axis) + lax.axis_index(axis)
    return index


def from_behind(array, axes, by):
    size = group_size(axes)
    pairs = [(i, i + by) for i in range(size) if 0 <= i + by < size]
    return lax.ppermute(array, axes, pairs)


def scatter_sum(total, axes):
    size = group_size(axes)
    own = group_index(axes)
    pieces = total.reshape(size, total.shape[0] // size, *total.shape[1:])
    summed = lax.dynamic_index_in_dim(pieces, own, 0, keepdims=False)
    for shift in range(1, size):
        piece = lax.dynamic_index_in_dim(pieces, (own + shift) % size, 0, keepdims=False)
        moved = lax.ppermute(piece.astype(jnp.bfloat16), axes, [(i, (i + shift) % size) for i in range(size)])
        summed = summed + moved.astype(jnp.float32)
    return summed


def halving_sum(total, axes):
    size = group_size(axes)
    own = group_index(axes)
    step = size // 2
    while step >= 1:
        halves = total.reshape(2, total.shape[0] // 2, *total.shape[1:])
        keep = (own // step) % 2
        kept = lax.dynamic_index_in_dim(halves, keep, 0, keepdims=False)
        given = lax.dynamic_index_in_dim(halves, 1 - keep, 0, keepdims=False)
        total = kept + lax.ppermute(given, axes, [(i, i ^ step) for i in range(size)])
        step //= 2
    return total


def everyone_sum(total, axes):
    size = group_size(axes)
    step = 1
    while step < size:
        total = total + lax.ppermute(total, axes, [(i, i ^ step) for i in range(size)])
        step *= 2
    return total


def near_sum(term, by_exchange):
    own_core = lax.axis_index("core")
    halves = term.reshape(term.shape[0], 2, term.shape[1] // 2)
    kept = lax.dynamic_index_in_dim(halves, own_core, 1, keepdims=False)
    given = lax.dynamic_index_in_dim(halves, 1 - own_core, 1, keepdims=False)
    moved = lax.ppermute(given.astype(jnp.bfloat16), "core", [(0, 1), (1, 0)])
    term = kept + moved.astype(jnp.float32)
    if not by_exchange:
        return scatter_sum(term, ("x",))
    size = lax.axis_size("x")
    pieces = term.reshape(size, term.shape[0] // size, term.shape[1]).astype(jnp.bfloat16)
    return lax.all_to_all(pieces, "x", 0, 0, tiled=True).astype(jnp.float32).sum(0)


def far_sum(term):
    lo_size = lax.axis_size("z_lo")
    hi_size = lax.axis_size("y") * lax.axis_size("z_hi")
    core_size = lax.axis_size("core")
    rows = term.reshape(lo_size, hi_size, term.shape[1]).transpose(1, 0, 2)
    rows = rows.reshape(hi_size * lo_size, 1, term.shape[1])
    row = lax.all_to_all(rows.astype(jnp.bfloat16), ("y", "z_hi", "z_lo"), 0, 0, tiled=True)
    row = row.astype(jnp.float32).sum(0)
    spread = jnp.broadcast_to(row[None], (hi_size * core_size, *row.shape))
    gathered = lax.all_to_all(spread, ("y", "z_hi", "core"), 0, 0, tiled=True)
    return gathered.reshape(hi_size, core_size, term.shape[1])


def gating(current, earlier, w_past, w_now):
    preact = jnp.dot(earlier, w_past, preferred_element_type=jnp.float32) + jnp.dot(
        current, w_now, preferred_element_type=jnp.float32
    )
    half_width = preact.shape[1] // 2
    return (jnp.tanh(preact[:, :half_width]), jax.nn.sigmoid(preact[:, half_width:]))


def fetch_past(series, layer_at):
    if layer_at == 0:
        return from_behind(series, EVERY, 1)
    return from_behind(series, OUTER, 2)


def return_past(series, layer_at):
    if layer_at == 0:
        return from_behind(series, EVERY, -1)
    return from_behind(series, OUTER, -2)


def layer_term(operands, grad_scale):
    earlier, current, gated_out, grad_preact, upstream = operands

    def contract(left_op, right_op):
        return lax.dot_general(
            left_op, right_op, (((0,), (0,)), ((), ())), preferred_element_type=jnp.float32
        )

    return (
        jnp.concatenate(
            [
                contract(earlier, grad_preact),
                contract(current, grad_preact),
                contract(gated_out, upstream),
            ],
            1,
        )
        * grad_scale
    )


def local(signal, conv_past, conv_now, out_proj, cotangent):
    gate_width = conv_past.shape[2]
    tick_count = signal.shape[0] * group_size(EVERY)
    grad_scale = 1.0 / math.sqrt(tick_count)
    layer_count = conv_past.shape[0]
    inputs, earliers, saved = ([], [], [])
    current = signal
    for layer_at in range(layer_count):
        earlier = fetch_past(current, layer_at)
        tanh_part, sig_part = gating(current, earlier, conv_past[layer_at], conv_now[layer_at])
        gated_out = (tanh_part * sig_part).astype(jnp.bfloat16)
        inputs.append(current)
        earliers.append(earlier)
        saved.append((tanh_part, sig_part, gated_out))
        current = (
            current.astype(jnp.float32)
            + jnp.dot(gated_out, out_proj[layer_at], preferred_element_type=jnp.float32)
        ).astype(jnp.bfloat16)
    result = current
    upstream = cotangent
    near_list = [None] * layer_count
    for layer_at in reversed(range(layer_count)):
        current = inputs[layer_at]
        earlier = earliers[layer_at]
        tanh_part, sig_part, gated_out = saved[layer_at]
        grad_gated = jnp.dot(upstream, out_proj[layer_at].T, preferred_element_type=jnp.float32)
        grad_filter = grad_gated * sig_part * (1.0 - tanh_part * tanh_part)
        grad_gate = grad_gated * tanh_part * sig_part * (1.0 - sig_part)
        grad_preact = jnp.concatenate([grad_filter, grad_gate], 1).astype(jnp.bfloat16)
        sent_back = jnp.dot(
            grad_preact, conv_past[layer_at].T, preferred_element_type=jnp.float32
        ).astype(jnp.bfloat16)
        arrived = return_past(sent_back, layer_at)
        operands = (earlier, current, gated_out, grad_preact, upstream)
        near_list[layer_at] = near_sum(layer_term(operands, grad_scale), True)
        if layer_at > 0:
            near_list, arrived = lax.optimization_barrier((near_list, arrived))
        local_grad = upstream.astype(jnp.float32) + jnp.dot(
            grad_preact, conv_now[layer_at].T, preferred_element_type=jnp.float32
        )
        upstream = (local_grad + arrived.astype(jnp.float32)).astype(jnp.bfloat16)
    whole = far_sum(jnp.concatenate(near_list, 1))
    half_width = near_list[0].shape[1]
    summed_list = [
        whole[:, :, layer_at * half_width : (layer_at + 1) * half_width].reshape(
            whole.shape[0], 2 * half_width
        )
        for layer_at in range(layer_count)
    ]
    past_list = [summed[:, :gate_width] for summed in summed_list]
    now_list = [summed[:, gate_width : 2 * gate_width] for summed in summed_list]
    out_list = [summed[:, 2 * gate_width :] for summed in summed_list]
    return (result, upstream, jnp.stack(past_list), jnp.stack(now_list), jnp.stack(out_list))


def solution(mesh):
    outer_size = mesh.shape["outer"]
    inner_size = mesh.shape["inner"]
    split = Mesh(
        mesh.devices.reshape(outer_size // 4, 2, 2, inner_size // 8, 8),
        ("y", "z_hi", "core", "x", "z_lo"),
    )
    placed = (P(EVERY, None), P(), P(), P(), P(EVERY, None))
    return jax.shard_map(
        local,
        mesh=split,
        in_specs=placed,
        out_specs=(
            P(EVERY, None),
            P(EVERY, None),
            P(None, INNER, None),
            P(None, INNER, None),
            P(None, INNER, None),
        ),
        check_vma=False,
    )
```

```python
import math

import jax
import jax.numpy as jnp
from jax import lax
from jax.sharding import Mesh
from jax.sharding import PartitionSpec as P

OUTER = ("y", "z_hi", "core")
INNER = ("x", "z_lo")
EVERY = OUTER + INNER


def group_size(axes):
    size = 1
    for axis in axes:
        size *= lax.axis_size(axis)
    return size


def group_index(axes):
    index = 0
    for axis in axes:
        index = index * lax.axis_size(axis) + lax.axis_index(axis)
    return index


def from_behind(array, axes, by):
    size = group_size(axes)
    pairs = [(i, i + by) for i in range(size) if 0 <= i + by < size]
    return lax.ppermute(array, axes, pairs)


def scatter_sum(total, axes):
    size = group_size(axes)
    own = group_index(axes)
    pieces = total.reshape(size, total.shape[0] // size, *total.shape[1:])
    summed = lax.dynamic_index_in_dim(pieces, own, 0, keepdims=False)
    for shift in range(1, size):
        piece = lax.dynamic_index_in_dim(pieces, (own + shift) % size, 0, keepdims=False)
        moved = lax.ppermute(piece.astype(jnp.bfloat16), axes, [(i, (i + shift) % size) for i in range(size)])
        summed = summed + moved.astype(jnp.float32)
    return summed


def halving_sum(total, axes):
    size = group_size(axes)
    own = group_index(axes)
    step = size // 2
    while step >= 1:
        halves = total.reshape(2, total.shape[0] // 2, *total.shape[1:])
        keep = (own // step) % 2
        kept = lax.dynamic_index_in_dim(halves, keep, 0, keepdims=False)
        given = lax.dynamic_index_in_dim(halves, 1 - keep, 0, keepdims=False)
        total = kept + lax.ppermute(given, axes, [(i, i ^ step) for i in range(size)])
        step //= 2
    return total


def everyone_sum(total, axes):
    size = group_size(axes)
    step = 1
    while step < size:
        total = total + lax.ppermute(total, axes, [(i, i ^ step) for i in range(size)])
        step *= 2
    return total


def near_sum(term, by_exchange):
    own_core = lax.axis_index("core")
    halves = term.reshape(term.shape[0], 2, term.shape[1] // 2)
    kept = lax.dynamic_index_in_dim(halves, own_core, 1, keepdims=False)
    given = lax.dynamic_index_in_dim(halves, 1 - own_core, 1, keepdims=False)
    moved = lax.ppermute(given.astype(jnp.bfloat16), "core", [(0, 1), (1, 0)])
    term = kept + moved.astype(jnp.float32)
    if not by_exchange:
        return scatter_sum(term, ("x",))
    size = lax.axis_size("x")
    pieces = term.reshape(size, term.shape[0] // size, term.shape[1]).astype(jnp.bfloat16)
    return lax.all_to_all(pieces, "x", 0, 0, tiled=True).astype(jnp.float32).sum(0)


def far_sum(term):
    lo_size = lax.axis_size("z_lo")
    hi_size = lax.axis_size("y") * lax.axis_size("z_hi")
    core_size = lax.axis_size("core")
    rows = term.reshape(lo_size, hi_size, term.shape[1]).transpose(1, 0, 2)
    rows = rows.reshape(hi_size * lo_size, 1, term.shape[1])
    row = lax.all_to_all(rows.astype(jnp.bfloat16), ("y", "z_hi", "z_lo"), 0, 0, tiled=True)
    row = row.astype(jnp.float32).sum(0)
    gathered = lax.all_gather(row, ("y", "z_hi", "core"), axis=0, tiled=False)
    return gathered.reshape(hi_size, core_size, term.shape[1])


def gating(current, earlier, w_past, w_now):
    preact = jnp.dot(earlier, w_past, preferred_element_type=jnp.float32) + jnp.dot(
        current, w_now, preferred_element_type=jnp.float32
    )
    half_width = preact.shape[1] // 2
    return (jnp.tanh(preact[:, :half_width]), jax.nn.sigmoid(preact[:, half_width:]))


def fetch_past(series, layer_at):
    if layer_at == 0:
        return from_behind(series, EVERY, 1)
    return from_behind(series, OUTER, 2)


def return_past(series, layer_at):
    if layer_at == 0:
        return from_behind(series, EVERY, -1)
    return from_behind(series, OUTER, -2)


def layer_term(operands, grad_scale):
    earlier, current, gated_out, grad_preact, upstream = operands

    def contract(left_op, right_op):
        return lax.dot_general(
            left_op, right_op, (((0,), (0,)), ((), ())), preferred_element_type=jnp.float32
        )

    return (
        jnp.concatenate(
            [
                contract(earlier, grad_preact),
                contract(current, grad_preact),
                contract(gated_out, upstream),
            ],
            1,
        )
        * grad_scale
    )


def local(signal, conv_past, conv_now, out_proj, cotangent):
    gate_width = conv_past.shape[2]
    tick_count = signal.shape[0] * group_size(EVERY)
    grad_scale = 1.0 / math.sqrt(tick_count)
    layer_count = conv_past.shape[0]
    inputs, earliers, saved = ([], [], [])
    current = signal
    for layer_at in range(layer_count):
        earlier = fetch_past(current, layer_at)
        tanh_part, sig_part = gating(current, earlier, conv_past[layer_at], conv_now[layer_at])
        gated_out = (tanh_part * sig_part).astype(jnp.bfloat16)
        inputs.append(current)
        earliers.append(earlier)
        saved.append((tanh_part, sig_part, gated_out))
        current = (
            current.astype(jnp.float32)
            + jnp.dot(gated_out, out_proj[layer_at], preferred_element_type=jnp.float32)
        ).astype(jnp.bfloat16)
    result = current
    upstream = cotangent
    near_list = [None] * layer_count
    for layer_at in reversed(range(layer_count)):
        current = inputs[layer_at]
        earlier = earliers[layer_at]
        tanh_part, sig_part, gated_out = saved[layer_at]
        grad_gated = jnp.dot(upstream, out_proj[layer_at].T, preferred_element_type=jnp.float32)
        grad_filter = grad_gated * sig_part * (1.0 - tanh_part * tanh_part)
        grad_gate = grad_gated * tanh_part * sig_part * (1.0 - sig_part)
        grad_preact = jnp.concatenate([grad_filter, grad_gate], 1).astype(jnp.bfloat16)
        sent_back = jnp.dot(
            grad_preact, conv_past[layer_at].T, preferred_element_type=jnp.float32
        ).astype(jnp.bfloat16)
        arrived = return_past(sent_back, layer_at)
        operands = (earlier, current, gated_out, grad_preact, upstream)
        near_list[layer_at] = near_sum(layer_term(operands, grad_scale), layer_at == 0)
        if layer_at > 0:
            near_list, arrived = lax.optimization_barrier((near_list, arrived))
        local_grad = upstream.astype(jnp.float32) + jnp.dot(
            grad_preact, conv_now[layer_at].T, preferred_element_type=jnp.float32
        )
        upstream = (local_grad + arrived.astype(jnp.float32)).astype(jnp.bfloat16)
    whole = far_sum(jnp.concatenate(near_list, 1))
    half_width = near_list[0].shape[1]
    summed_list = [
        whole[:, :, layer_at * half_width : (layer_at + 1) * half_width].reshape(
            whole.shape[0], 2 * half_width
        )
        for layer_at in range(layer_count)
    ]
    past_list = [summed[:, :gate_width] for summed in summed_list]
    now_list = [summed[:, gate_width : 2 * gate_width] for summed in summed_list]
    out_list = [summed[:, 2 * gate_width :] for summed in summed_list]
    return (result, upstream, jnp.stack(past_list), jnp.stack(now_list), jnp.stack(out_list))


def solution(mesh):
    outer_size = mesh.shape["outer"]
    inner_size = mesh.shape["inner"]
    split = Mesh(
        mesh.devices.reshape(outer_size // 4, 2, 2, inner_size // 8, 8),
        ("y", "z_hi", "core", "x", "z_lo"),
    )
    placed = (P(EVERY, None), P(), P(), P(), P(EVERY, None))
    return jax.shard_map(
        local,
        mesh=split,
        in_specs=placed,
        out_specs=(
            P(EVERY, None),
            P(EVERY, None),
            P(None, INNER, None),
            P(None, INNER, None),
            P(None, INNER, None),
        ),
        check_vma=False,
    )
```

```python
import math

import jax
import jax.numpy as jnp
from jax import lax
from jax.sharding import Mesh
from jax.sharding import PartitionSpec as P

OUTER = ("y", "z_hi", "core")
INNER = ("x", "z_lo")
EVERY = OUTER + INNER


def group_size(axes):
    size = 1
    for axis in axes:
        size *= lax.axis_size(axis)
    return size


def group_index(axes):
    index = 0
    for axis in axes:
        index = index * lax.axis_size(axis) + lax.axis_index(axis)
    return index


def from_behind(array, axes, by):
    size = group_size(axes)
    pairs = [(i, i + by) for i in range(size) if 0 <= i + by < size]
    return lax.ppermute(array, axes, pairs)


def scatter_sum(total, axes):
    size = group_size(axes)
    own = group_index(axes)
    pieces = total.reshape(size, total.shape[0] // size, *total.shape[1:])
    summed = lax.dynamic_index_in_dim(pieces, own, 0, keepdims=False)
    for shift in range(1, size):
        piece = lax.dynamic_index_in_dim(pieces, (own + shift) % size, 0, keepdims=False)
        moved = lax.ppermute(piece.astype(jnp.bfloat16), axes, [(i, (i + shift) % size) for i in range(size)])
        summed = summed + moved.astype(jnp.float32)
    return summed


def halving_sum(total, axes):
    size = group_size(axes)
    own = group_index(axes)
    step = size // 2
    while step >= 1:
        halves = total.reshape(2, total.shape[0] // 2, *total.shape[1:])
        keep = (own // step) % 2
        kept = lax.dynamic_index_in_dim(halves, keep, 0, keepdims=False)
        given = lax.dynamic_index_in_dim(halves, 1 - keep, 0, keepdims=False)
        total = kept + lax.ppermute(given, axes, [(i, i ^ step) for i in range(size)])
        step //= 2
    return total


def everyone_sum(total, axes):
    size = group_size(axes)
    step = 1
    while step < size:
        total = total + lax.ppermute(total, axes, [(i, i ^ step) for i in range(size)])
        step *= 2
    return total


def near_sum(term, by_exchange):
    own_core = lax.axis_index("core")
    halves = term.reshape(term.shape[0], 2, term.shape[1] // 2)
    kept = lax.dynamic_index_in_dim(halves, own_core, 1, keepdims=False)
    given = lax.dynamic_index_in_dim(halves, 1 - own_core, 1, keepdims=False)
    moved = lax.ppermute(given.astype(jnp.bfloat16), "core", [(0, 1), (1, 0)])
    term = kept + moved.astype(jnp.float32)
    if not by_exchange:
        return scatter_sum(term, ("x",))
    size = lax.axis_size("x")
    pieces = term.reshape(size, term.shape[0] // size, term.shape[1]).astype(jnp.bfloat16)
    return lax.all_to_all(pieces, "x", 0, 0, tiled=True).astype(jnp.float32).sum(0)


def far_sum(term):
    lo_size = lax.axis_size("z_lo")
    hi_size = lax.axis_size("y") * lax.axis_size("z_hi")
    core_size = lax.axis_size("core")
    rows = term.reshape(lo_size, hi_size, term.shape[1]).transpose(1, 0, 2)
    rows = rows.reshape(hi_size * lo_size, 1, term.shape[1])
    row = lax.all_to_all(rows.astype(jnp.bfloat16), ("y", "z_hi", "z_lo"), 0, 0, tiled=True)
    row = row.astype(jnp.float32).sum(0)
    spread = jnp.broadcast_to(row[None], (hi_size * core_size, *row.shape))
    gathered = lax.all_to_all(spread, ("y", "z_hi", "core"), 0, 0, tiled=True)
    return gathered.reshape(hi_size, core_size, term.shape[1])


def gating(current, earlier, w_past, w_now):
    preact = jnp.dot(earlier, w_past, preferred_element_type=jnp.float32) + jnp.dot(
        current, w_now, preferred_element_type=jnp.float32
    )
    half_width = preact.shape[1] // 2
    return (jnp.tanh(preact[:, :half_width]), jax.nn.sigmoid(preact[:, half_width:]))


def fetch_past(series, layer_at):
    if layer_at == 0:
        return from_behind(series, EVERY, 1)
    return from_behind(series, OUTER, 2)


def return_past(series, layer_at):
    if layer_at == 0:
        return from_behind(series, EVERY, -1)
    return from_behind(series, OUTER, -2)


def layer_term(operands, grad_scale):
    earlier, current, gated_out, grad_preact, upstream = operands

    def contract(left_op, right_op):
        return lax.dot_general(
            left_op, right_op, (((0,), (0,)), ((), ())), preferred_element_type=jnp.float32
        )

    return (
        jnp.concatenate(
            [
                contract(earlier, grad_preact),
                contract(current, grad_preact),
                contract(gated_out, upstream),
            ],
            1,
        )
        * grad_scale
    )


def local(signal, conv_past, conv_now, out_proj, cotangent):
    gate_width = conv_past.shape[2]
    tick_count = signal.shape[0] * group_size(EVERY)
    grad_scale = 1.0 / math.sqrt(tick_count)
    layer_count = conv_past.shape[0]
    inputs, earliers, saved = ([], [], [])
    current = signal
    for layer_at in range(layer_count):
        earlier = fetch_past(current, layer_at)
        tanh_part, sig_part = gating(current, earlier, conv_past[layer_at], conv_now[layer_at])
        gated_out = (tanh_part * sig_part).astype(jnp.bfloat16)
        inputs.append(current)
        earliers.append(earlier)
        saved.append((tanh_part, sig_part, gated_out))
        current = (
            current.astype(jnp.float32)
            + jnp.dot(gated_out, out_proj[layer_at], preferred_element_type=jnp.float32)
        ).astype(jnp.bfloat16)
    result = current
    upstream = cotangent
    near_list = [None] * layer_count
    for layer_at in reversed(range(layer_count)):
        current = inputs[layer_at]
        earlier = earliers[layer_at]
        tanh_part, sig_part, gated_out = saved[layer_at]
        grad_gated = jnp.dot(upstream, out_proj[layer_at].T, preferred_element_type=jnp.float32)
        grad_filter = grad_gated * sig_part * (1.0 - tanh_part * tanh_part)
        grad_gate = grad_gated * tanh_part * sig_part * (1.0 - sig_part)
        grad_preact = jnp.concatenate([grad_filter, grad_gate], 1).astype(jnp.bfloat16)
        sent_back = jnp.dot(
            grad_preact, conv_past[layer_at].T, preferred_element_type=jnp.float32
        ).astype(jnp.bfloat16)
        arrived = return_past(sent_back, layer_at)
        operands = (earlier, current, gated_out, grad_preact, upstream)
        near_list[layer_at] = near_sum(layer_term(operands, grad_scale), layer_at == 0)
        local_grad = upstream.astype(jnp.float32) + jnp.dot(
            grad_preact, conv_now[layer_at].T, preferred_element_type=jnp.float32
        )
        upstream = (local_grad + arrived.astype(jnp.float32)).astype(jnp.bfloat16)
    whole = far_sum(jnp.concatenate(near_list, 1))
    half_width = near_list[0].shape[1]
    summed_list = [
        whole[:, :, layer_at * half_width : (layer_at + 1) * half_width].reshape(
            whole.shape[0], 2 * half_width
        )
        for layer_at in range(layer_count)
    ]
    past_list = [summed[:, :gate_width] for summed in summed_list]
    now_list = [summed[:, gate_width : 2 * gate_width] for summed in summed_list]
    out_list = [summed[:, 2 * gate_width :] for summed in summed_list]
    return (result, upstream, jnp.stack(past_list), jnp.stack(now_list), jnp.stack(out_list))


def solution(mesh):
    outer_size = mesh.shape["outer"]
    inner_size = mesh.shape["inner"]
    split = Mesh(
        mesh.devices.reshape(outer_size // 4, 2, 2, inner_size // 8, 8),
        ("y", "z_hi", "core", "x", "z_lo"),
    )
    placed = (P(EVERY, None), P(), P(), P(), P(EVERY, None))
    return jax.shard_map(
        local,
        mesh=split,
        in_specs=placed,
        out_specs=(
            P(EVERY, None),
            P(EVERY, None),
            P(None, INNER, None),
            P(None, INNER, None),
            P(None, INNER, None),
        ),
        check_vma=False,
    )
```

```python
import math

import jax
import jax.numpy as jnp
from jax import lax
from jax.sharding import Mesh
from jax.sharding import PartitionSpec as P

OUTER = ("y", "z_hi", "core")
INNER = ("x", "z_lo")
EVERY = OUTER + INNER


def group_size(axes):
    size = 1
    for axis in axes:
        size *= lax.axis_size(axis)
    return size


def group_index(axes):
    index = 0
    for axis in axes:
        index = index * lax.axis_size(axis) + lax.axis_index(axis)
    return index


def from_behind(array, axes, by):
    size = group_size(axes)
    pairs = [(i, i + by) for i in range(size) if 0 <= i + by < size]
    return lax.ppermute(array, axes, pairs)


def scatter_sum(total, axes):
    size = group_size(axes)
    own = group_index(axes)
    pieces = total.reshape(size, total.shape[0] // size, *total.shape[1:])
    summed = lax.dynamic_index_in_dim(pieces, own, 0, keepdims=False)
    for shift in range(1, size):
        piece = lax.dynamic_index_in_dim(pieces, (own + shift) % size, 0, keepdims=False)
        moved = lax.ppermute(piece.astype(jnp.bfloat16), axes, [(i, (i + shift) % size) for i in range(size)])
        summed = summed + moved.astype(jnp.float32)
    return summed


def halving_sum(total, axes):
    size = group_size(axes)
    own = group_index(axes)
    step = size // 2
    while step >= 1:
        halves = total.reshape(2, total.shape[0] // 2, *total.shape[1:])
        keep = (own // step) % 2
        kept = lax.dynamic_index_in_dim(halves, keep, 0, keepdims=False)
        given = lax.dynamic_index_in_dim(halves, 1 - keep, 0, keepdims=False)
        total = kept + lax.ppermute(given, axes, [(i, i ^ step) for i in range(size)])
        step //= 2
    return total


def everyone_sum(total, axes):
    size = group_size(axes)
    step = 1
    while step < size:
        total = total + lax.ppermute(total, axes, [(i, i ^ step) for i in range(size)])
        step *= 2
    return total


def near_sum(term, by_exchange):
    own_core = lax.axis_index("core")
    halves = term.reshape(term.shape[0], 2, term.shape[1] // 2)
    kept = lax.dynamic_index_in_dim(halves, own_core, 1, keepdims=False)
    given = lax.dynamic_index_in_dim(halves, 1 - own_core, 1, keepdims=False)
    moved = lax.ppermute(given.astype(jnp.bfloat16), "core", [(0, 1), (1, 0)])
    term = kept + moved.astype(jnp.float32)
    if not by_exchange:
        return scatter_sum(term, ("x",))
    size = lax.axis_size("x")
    pieces = term.reshape(size, term.shape[0] // size, term.shape[1]).astype(jnp.bfloat16)
    return lax.all_to_all(pieces, "x", 0, 0, tiled=True).astype(jnp.float32).sum(0)


def far_sum(term):
    lo_size = lax.axis_size("z_lo")
    hi_size = lax.axis_size("y") * lax.axis_size("z_hi")
    core_size = lax.axis_size("core")
    rows = term.reshape(lo_size, hi_size, term.shape[1]).transpose(1, 0, 2)
    rows = rows.reshape(hi_size * lo_size, 1, term.shape[1])
    row = lax.all_to_all(rows.astype(jnp.bfloat16), ("y", "z_hi", "z_lo"), 0, 0, tiled=True)
    row = row.astype(jnp.float32).sum(0)
    spread = jnp.broadcast_to(row[None], (hi_size * core_size, *row.shape))
    gathered = lax.all_to_all(spread, ("y", "z_hi", "core"), 0, 0, tiled=True)
    return gathered.reshape(hi_size, core_size, term.shape[1])


def gating(current, earlier, w_past, w_now):
    preact = jnp.dot(earlier, w_past, preferred_element_type=jnp.float32) + jnp.dot(
        current, w_now, preferred_element_type=jnp.float32
    )
    half_width = preact.shape[1] // 2
    return (jnp.tanh(preact[:, :half_width]), jax.nn.sigmoid(preact[:, half_width:]))


def fetch_past(series, layer_at):
    if layer_at == 0:
        return from_behind(series, EVERY, 1)
    return from_behind(series, OUTER, 2)


def return_past(series, layer_at):
    if layer_at == 0:
        return from_behind(series, EVERY, -1)
    return from_behind(series, OUTER, -2)


def layer_term(operands, grad_scale):
    earlier, current, gated_out, grad_preact, upstream = operands

    def contract(left_op, right_op):
        return lax.dot_general(
            left_op, right_op, (((0,), (0,)), ((), ())), preferred_element_type=jnp.float32
        )

    return (
        jnp.concatenate(
            [
                contract(earlier, grad_preact),
                contract(current, grad_preact),
                contract(gated_out, upstream),
            ],
            1,
        )
        * grad_scale
    )


def local(signal, conv_past, conv_now, out_proj, cotangent):
    gate_width = conv_past.shape[2]
    tick_count = signal.shape[0] * group_size(EVERY)
    grad_scale = 1.0 / math.sqrt(tick_count)
    layer_count = conv_past.shape[0]
    inputs, earliers, saved = ([], [], [])
    current = signal
    for layer_at in range(layer_count):
        earlier = fetch_past(current, layer_at)
        tanh_part, sig_part = gating(current, earlier, conv_past[layer_at], conv_now[layer_at])
        gated_out = (tanh_part * sig_part).astype(jnp.bfloat16)
        inputs.append(current)
        earliers.append(earlier)
        saved.append((tanh_part, sig_part, gated_out))
        current = (
            current.astype(jnp.float32)
            + jnp.dot(gated_out, out_proj[layer_at], preferred_element_type=jnp.float32)
        ).astype(jnp.bfloat16)
    result = current
    upstream = cotangent
    near_list = [None] * layer_count
    for layer_at in reversed(range(layer_count)):
        current = inputs[layer_at]
        earlier = earliers[layer_at]
        tanh_part, sig_part, gated_out = saved[layer_at]
        grad_gated = jnp.dot(upstream, out_proj[layer_at].T, preferred_element_type=jnp.float32)
        grad_filter = grad_gated * sig_part * (1.0 - tanh_part * tanh_part)
        grad_gate = grad_gated * tanh_part * sig_part * (1.0 - sig_part)
        grad_preact = jnp.concatenate([grad_filter, grad_gate], 1).astype(jnp.bfloat16)
        sent_back = jnp.dot(
            grad_preact, conv_past[layer_at].T, preferred_element_type=jnp.float32
        ).astype(jnp.bfloat16)
        arrived = return_past(sent_back, layer_at)
        operands = (earlier, current, gated_out, grad_preact, upstream)
        near_list[layer_at] = near_sum(layer_term(operands, grad_scale), layer_at == 0)
        near_list, arrived = lax.optimization_barrier((near_list, arrived))
        local_grad = upstream.astype(jnp.float32) + jnp.dot(
            grad_preact, conv_now[layer_at].T, preferred_element_type=jnp.float32
        )
        upstream = (local_grad + arrived.astype(jnp.float32)).astype(jnp.bfloat16)
    whole = far_sum(jnp.concatenate(near_list, 1))
    half_width = near_list[0].shape[1]
    summed_list = [
        whole[:, :, layer_at * half_width : (layer_at + 1) * half_width].reshape(
            whole.shape[0], 2 * half_width
        )
        for layer_at in range(layer_count)
    ]
    past_list = [summed[:, :gate_width] for summed in summed_list]
    now_list = [summed[:, gate_width : 2 * gate_width] for summed in summed_list]
    out_list = [summed[:, 2 * gate_width :] for summed in summed_list]
    return (result, upstream, jnp.stack(past_list), jnp.stack(now_list), jnp.stack(out_list))


def solution(mesh):
    outer_size = mesh.shape["outer"]
    inner_size = mesh.shape["inner"]
    split = Mesh(
        mesh.devices.reshape(outer_size // 4, 2, 2, inner_size // 8, 8),
        ("y", "z_hi", "core", "x", "z_lo"),
    )
    placed = (P(EVERY, None), P(), P(), P(), P(EVERY, None))
    return jax.shard_map(
        local,
        mesh=split,
        in_specs=placed,
        out_specs=(
            P(EVERY, None),
            P(EVERY, None),
            P(None, INNER, None),
            P(None, INNER, None),
            P(None, INNER, None),
        ),
        check_vma=False,
    )
```

```python
import math

import jax
import jax.numpy as jnp
from jax import lax
from jax.sharding import Mesh
from jax.sharding import PartitionSpec as P

OUTER = ("y", "z_hi", "core")
INNER = ("x", "z_lo")
EVERY = OUTER + INNER


def group_size(axes):
    size = 1
    for axis in axes:
        size *= lax.axis_size(axis)
    return size


def group_index(axes):
    index = 0
    for axis in axes:
        index = index * lax.axis_size(axis) + lax.axis_index(axis)
    return index


def from_behind(array, axes, by):
    size = group_size(axes)
    pairs = [(i, i + by) for i in range(size) if 0 <= i + by < size]
    return lax.ppermute(array, axes, pairs)


def scatter_sum(total, axes):
    size = group_size(axes)
    own = group_index(axes)
    pieces = total.reshape(size, total.shape[0] // size, *total.shape[1:])
    summed = lax.dynamic_index_in_dim(pieces, own, 0, keepdims=False)
    for shift in range(1, size):
        piece = lax.dynamic_index_in_dim(pieces, (own + shift) % size, 0, keepdims=False)
        moved = lax.ppermute(piece.astype(jnp.bfloat16), axes, [(i, (i + shift) % size) for i in range(size)])
        summed = summed + moved.astype(jnp.float32)
    return summed


def halving_sum(total, axes):
    size = group_size(axes)
    own = group_index(axes)
    step = size // 2
    while step >= 1:
        halves = total.reshape(2, total.shape[0] // 2, *total.shape[1:])
        keep = (own // step) % 2
        kept = lax.dynamic_index_in_dim(halves, keep, 0, keepdims=False)
        given = lax.dynamic_index_in_dim(halves, 1 - keep, 0, keepdims=False)
        total = kept + lax.ppermute(given, axes, [(i, i ^ step) for i in range(size)])
        step //= 2
    return total


def everyone_sum(total, axes):
    size = group_size(axes)
    step = 1
    while step < size:
        total = total + lax.ppermute(total, axes, [(i, i ^ step) for i in range(size)])
        step *= 2
    return total


def near_sum(term, by_exchange):
    if by_exchange:
        core_size = lax.axis_size("core")
        x_size = lax.axis_size("x")
        pieces = term.reshape(x_size, term.shape[0] // x_size, core_size, term.shape[1] // core_size)
        pieces = pieces.transpose(2, 0, 1, 3).reshape(core_size * x_size, term.shape[0] // x_size, -1)
        moved = lax.all_to_all(pieces.astype(jnp.bfloat16), ("core", "x"), 0, 0, tiled=True)
        return moved.astype(jnp.float32).sum(0)
    own_core = lax.axis_index("core")
    halves = term.reshape(term.shape[0], 2, term.shape[1] // 2)
    kept = lax.dynamic_index_in_dim(halves, own_core, 1, keepdims=False)
    given = lax.dynamic_index_in_dim(halves, 1 - own_core, 1, keepdims=False)
    moved = lax.ppermute(given.astype(jnp.bfloat16), "core", [(0, 1), (1, 0)])
    return scatter_sum(kept + moved.astype(jnp.float32), ("x",))


def far_sum(term):
    lo_size = lax.axis_size("z_lo")
    hi_size = lax.axis_size("y") * lax.axis_size("z_hi")
    core_size = lax.axis_size("core")
    rows = term.reshape(lo_size, hi_size, term.shape[1]).transpose(1, 0, 2)
    rows = rows.reshape(hi_size * lo_size, 1, term.shape[1])
    row = lax.all_to_all(rows.astype(jnp.bfloat16), ("y", "z_hi", "z_lo"), 0, 0, tiled=True)
    row = row.astype(jnp.float32).sum(0)
    spread = jnp.broadcast_to(row[None], (hi_size * core_size, *row.shape))
    gathered = lax.all_to_all(spread, ("y", "z_hi", "core"), 0, 0, tiled=True)
    return gathered.reshape(hi_size, core_size, term.shape[1])


def gating(current, earlier, w_past, w_now):
    preact = jnp.dot(earlier, w_past, preferred_element_type=jnp.float32) + jnp.dot(
        current, w_now, preferred_element_type=jnp.float32
    )
    half_width = preact.shape[1] // 2
    return (jnp.tanh(preact[:, :half_width]), jax.nn.sigmoid(preact[:, half_width:]))


def fetch_past(series, layer_at):
    if layer_at == 0:
        return from_behind(series, EVERY, 1)
    return from_behind(series, OUTER, 2)


def return_past(series, layer_at):
    if layer_at == 0:
        return from_behind(series, EVERY, -1)
    return from_behind(series, OUTER, -2)


def layer_term(operands, grad_scale):
    earlier, current, gated_out, grad_preact, upstream = operands

    def contract(left_op, right_op):
        return lax.dot_general(
            left_op, right_op, (((0,), (0,)), ((), ())), preferred_element_type=jnp.float32
        )

    return (
        jnp.concatenate(
            [
                contract(earlier, grad_preact),
                contract(current, grad_preact),
                contract(gated_out, upstream),
            ],
            1,
        )
        * grad_scale
    )


def local(signal, conv_past, conv_now, out_proj, cotangent):
    gate_width = conv_past.shape[2]
    tick_count = signal.shape[0] * group_size(EVERY)
    grad_scale = 1.0 / math.sqrt(tick_count)
    layer_count = conv_past.shape[0]
    inputs, earliers, saved = ([], [], [])
    current = signal
    for layer_at in range(layer_count):
        earlier = fetch_past(current, layer_at)
        tanh_part, sig_part = gating(current, earlier, conv_past[layer_at], conv_now[layer_at])
        gated_out = (tanh_part * sig_part).astype(jnp.bfloat16)
        inputs.append(current)
        earliers.append(earlier)
        saved.append((tanh_part, sig_part, gated_out))
        current = (
            current.astype(jnp.float32)
            + jnp.dot(gated_out, out_proj[layer_at], preferred_element_type=jnp.float32)
        ).astype(jnp.bfloat16)
    result = current
    upstream = cotangent
    near_list = [None] * layer_count
    for layer_at in reversed(range(layer_count)):
        current = inputs[layer_at]
        earlier = earliers[layer_at]
        tanh_part, sig_part, gated_out = saved[layer_at]
        grad_gated = jnp.dot(upstream, out_proj[layer_at].T, preferred_element_type=jnp.float32)
        grad_filter = grad_gated * sig_part * (1.0 - tanh_part * tanh_part)
        grad_gate = grad_gated * tanh_part * sig_part * (1.0 - sig_part)
        grad_preact = jnp.concatenate([grad_filter, grad_gate], 1).astype(jnp.bfloat16)
        sent_back = jnp.dot(
            grad_preact, conv_past[layer_at].T, preferred_element_type=jnp.float32
        ).astype(jnp.bfloat16)
        arrived = return_past(sent_back, layer_at)
        operands = (earlier, current, gated_out, grad_preact, upstream)
        near_list[layer_at] = near_sum(layer_term(operands, grad_scale), True)
        if layer_at > 0:
            near_list, arrived = lax.optimization_barrier((near_list, arrived))
        local_grad = upstream.astype(jnp.float32) + jnp.dot(
            grad_preact, conv_now[layer_at].T, preferred_element_type=jnp.float32
        )
        upstream = (local_grad + arrived.astype(jnp.float32)).astype(jnp.bfloat16)
    whole = far_sum(jnp.concatenate(near_list, 1))
    half_width = near_list[0].shape[1]
    summed_list = [
        whole[:, :, layer_at * half_width : (layer_at + 1) * half_width].reshape(
            whole.shape[0], 2 * half_width
        )
        for layer_at in range(layer_count)
    ]
    past_list = [summed[:, :gate_width] for summed in summed_list]
    now_list = [summed[:, gate_width : 2 * gate_width] for summed in summed_list]
    out_list = [summed[:, 2 * gate_width :] for summed in summed_list]
    return (result, upstream, jnp.stack(past_list), jnp.stack(now_list), jnp.stack(out_list))


def solution(mesh):
    outer_size = mesh.shape["outer"]
    inner_size = mesh.shape["inner"]
    split = Mesh(
        mesh.devices.reshape(outer_size // 4, 2, 2, inner_size // 8, 8),
        ("y", "z_hi", "core", "x", "z_lo"),
    )
    placed = (P(EVERY, None), P(), P(), P(), P(EVERY, None))
    return jax.shard_map(
        local,
        mesh=split,
        in_specs=placed,
        out_specs=(
            P(EVERY, None),
            P(EVERY, None),
            P(None, INNER, None),
            P(None, INNER, None),
            P(None, INNER, None),
        ),
        check_vma=False,
    )
```
